128 devices in a mesh: dp: 8 (over x, core), table: 16 (over z, y).
Axes of the slice: x: 4, y: 4, z: 4, core: 2. Of those that a mesh axis runs over, the one named last changes fastest.
Arguments:
- user_table: bfloat16 [524288, 256], P(('dp', 'table')), may hold values from -6 to 6
- item_table: bfloat16 [524288, 256], P(('dp', 'table')), may hold values from -6 to 6
- hist_owner: int32 [262144, 1], P(('dp', 'table')), may hold values from 0 to 127; in each aligned block of 2048 rows (0 to 2047, 2048 to 4095, ...) at most 32 rows name the same one
- hist_row: int32 [262144], P(('dp', 'table')), may hold values from 0 to 4095
- hist_seg: int32 [128, 2048], P(('dp', 'table')), may hold values from 0 to 127, never falling along the last dimension, each value on 1 to 64 neighbouring positions
- hist_wix: int32 [262144], P(('dp', 'table')), may hold values from 0 to 63
- bag_weights: bfloat16 [64], replicated, may hold values from 0.099609375 to 1
- item_owner: int32 [16384, 1], P(('dp', 'table')), may hold values from 0 to 127; in each aligned block of 128 rows (0 to 127, 128 to 255, ...) at most 2 rows name the same one
- item_row: int32 [16384], P(('dp', 'table')), may hold values from 0 to 4095
- user_proj: bfloat16 [256, 256], replicated, may hold values from -0.375 to 0.375
- item_proj: bfloat16 [256, 256], replicated, may hold values from -0.375 to 0.375
- logit_scale: float32 [1], replicated, may hold values from 8 to 600
Outputs:
- user_grad: float32 [524288, 256], P(('dp', 'table'))
- item_grad: float32 [524288, 256], P(('dp', 'table'))
- user_proj_grad: float32 [256, 256], replicated
- item_proj_grad: float32 [256, 256], replicated
The draws below stay inside these ranges and needn't reach their ends.
Inputs may be any that keep to these rules, and one draw needn't show every extreme that they name: `hist_owner`: among the 2048 history ids of one device, no owner is named more than 32 times; some owner exactly 32 times. `item_owner`: among the 128 samples of one device, no owner is named more than 2 times; some owner exactly 2 times. `hist_seg`: each row numbers 128 samples in order; each sample has 1 to 64 ids, one has exactly 64.
All inputs are finite; a program needn't handle non-finite values.
Results may differ from the reference program's by a relative error of at most 0.01.
The reference program's roundings to bfloat16 on the way count: a program that leaves them out, or rounds other values in their place, can miss the bound.
Values may be sent and summed in bfloat16 or wider, within the bound.
No kernel may reach another device: no remote copies, remote signals or barrier semaphores. Data moves between devices by JAX's collectives and lax.ppermute only.
A program may use at most 128 MiB of HBM per device.

```python
import math
import jax
import jax.numpy as jnp
import numpy as np
from jax import lax

E = 256
ROWS_DEV = 4096
NW = 64
B_DEV = 128
BAG_MAX = 64
TOK_DEV = 2048
HIST = 262144
BATCH = 16384
VOCAB = 524288
CAP = 32
CAP_ITEM = 2
N_DP = 8
N_TABLE = 16


def draw_logit_scale(key, part):
    return jax.random.uniform(key, (1,), jnp.float32, 8.0, 20.0)


def plant(values, stream_key, low, top_value):
    longest = values.shape.index(max(values.shape))
    spots = []
    for shift in (0, 1):
        where = [jax.random.randint(jax.random.fold_in(stream_key, axis), (), 0, length) for axis, length in enumerate(values.shape)]
        where[longest] = (where[longest] + shift) % values.shape[longest]
        spots.append(tuple(where))
    return values.at[spots[0]].set(low).at[spots[1]].set(top_value)


def levels(key, dims, split, least, high):
    level, own = 1.0, jax.random.fold_in(key, 6)
    for position, parts in split:
        draws = jnp.exp(jax.random.uniform(jax.random.fold_in(own, position), (parts,), jnp.float32, least / len(split), high / len(split)))
        level = level * jnp.repeat(draws, dims[position] // parts).reshape([-1 if axis == position else 1 for axis in range(len(dims))])
    return level


def split_up(amount, total, most, slope):
    loads = [(1 << 20) // math.isqrt(rank ** slope) + 1 for rank in range(2, amount + 1)]
    surplus, given = total - most - (amount - 1), [1] * (amount - 1)
    while surplus > 0:
        movable = [i for i in range(amount - 1) if given[i] < most]
        pool, left = sum([loads[i] for i in movable]), surplus
        for i in movable:
            more = min(most - given[i], max(1, left * loads[i] // pool), surplus)
            given[i] = given[i] + more
            surplus = surplus - more
    return np.array([most] + given)


def ragged_sizes(key, amount, total, limit, slope):
    if amount == 2:
        one = jax.random.randint(key, (), max(1, total - limit), min(limit, total - 1) + 1)
        return jnp.stack([one, total - one])
    lengths = jnp.asarray(split_up(amount, total, limit, slope), jnp.int32)
    twos = (amount - 1) // 2
    source_of, taker = lengths[1:1 + 2 * twos:2], lengths[2:2 + 2 * twos:2]
    margin = jnp.minimum(source_of - 1, limit - taker)
    shifted = jax.random.randint(jax.random.fold_in(key, 1), (twos,), 0, 1 << 20) % (margin + 1)
    lengths = lengths.at[1:1 + 2 * twos:2].set(source_of - shifted).at[2:2 + 2 * twos:2].set(taker + shifted)
    return lengths[jax.random.permutation(jax.random.fold_in(key, 2), amount)]


def deal_out(stream_key, own, number, rows, number_of, top, bound, lean):
    ranking = jax.random.permutation(stream_key, number_of)
    crowded, usual = portions_of(number_of, rows * top, bound, lean, True), portions_of(number_of, rows * top, bound, lean, False)
    places = jnp.arange(number_of)

    def named(sizes, offset_by):
        used = int((sizes > 0).sum())
        fixed = max(1, used // 4)
        moved = fixed + (places - fixed + offset_by * (used - fixed)) % max(1, number_of - fixed)
        return jnp.zeros((number_of,), jnp.int32).at[ranking[jnp.where(places < fixed, places, moved)]].set(jnp.asarray(sizes, jnp.int32))

    sizes = jnp.where(number % 4 == 0, named(crowded, number // 4), named(usual, number - number // 4 - 1))
    mixed = jax.random.permutation(jax.random.fold_in(own, 3), number_of)
    giver, sink = mixed[0:number_of // 2 * 2:2], mixed[1:number_of // 2 * 2:2]
    slack = jnp.minimum(sizes[giver] - 1, bound - sizes[sink]) // 2
    slack = jnp.where((giver == ranking[0]) | (sink == ranking[0]) | (sizes[sink] == 0), 0, jnp.maximum(slack, 0))
    moved = jax.random.randint(jax.random.fold_in(own, 4), (number_of // 2,), 0, 1 << 20) % (slack + 1)
    sizes = sizes.at[giver].add(-moved).at[sink].add(moved)
    members = jnp.searchsorted(jnp.cumsum(sizes), jnp.arange(rows * top), side="right").astype(jnp.int32)
    listing = members.reshape(top, rows).T
    listing = listing[jax.random.permutation(jax.random.fold_in(own, 1), rows)]
    offset_by = jax.random.randint(jax.random.fold_in(own, 2), (rows, 1), 0, top)
    return jnp.take_along_axis(listing, (jnp.arange(top)[None, :] + offset_by) % top, axis=1)


def portions_of(amount, total, bound, lean, full):
    loads = [(1 << 20) // math.isqrt(standing ** lean) + 1 for standing in range(1, amount + 1)]
    largest = bound if full else min(bound, max(-(-total // amount), total * loads[0] // sum(loads)))
    least = 1 if total - largest >= amount - 1 else 0
    holding, surplus = [largest] + [least] * (amount - 1), total - largest - least * (amount - 1)
    while surplus > 0:
        candidates = [i for i in range(1, amount) if holding[i] < largest] or [i for i in range(1, amount) if holding[i] < bound]
        mass, remaining = sum([loads[i] for i in candidates]), surplus
        for i in candidates:
            more = min(bound - holding[i], max(1, remaining * loads[i] // mass), surplus)
            holding[i] = holding[i] + more
            surplus = surplus - more
    return np.array(holding)


def bell_draw(key, shape, spread, limit, pieces=(), kind=jnp.bfloat16):
    values = spread * jax.random.normal(key, shape, jnp.float32)
    if pieces:
        values = values * levels(key, shape, pieces, -0.22, 0.18)
    return jnp.clip(values, -limit, limit).astype(kind)


def setup_inputs(seed: int = 0) -> dict:
    key_list = jax.random.split(jax.random.key(seed), 13)
    user_table = bell_draw(key_list[0], (VOCAB, E), 1.0, 6.0, ((0, 128),))
    item_table = bell_draw(key_list[1], (VOCAB, E), 1.0, 6.0, ((0, 128),))
    hist_owner_keys = jax.random.split(jax.random.fold_in(key_list[2], 1), HIST // TOK_DEV)
    hist_owner_turns = jax.random.permutation(jax.random.fold_in(key_list[2], 3), HIST // TOK_DEV)
    hist_owner = jax.vmap(lambda own, number: deal_out(jax.random.fold_in(key_list[2], 2), own, number, TOK_DEV, N_DP * N_TABLE, 1, CAP, 2))(hist_owner_keys, hist_owner_turns).reshape((HIST, 1))
    hist_row = plant(jax.random.randint(key_list[3], (HIST,), 0, ROWS_DEV), jax.random.fold_in(key_list[3], 1), 0, ROWS_DEV - 1).astype(jnp.int32)
    hist_seg = jax.vmap(lambda own: jnp.searchsorted(jnp.cumsum(ragged_sizes(own, B_DEV, TOK_DEV, BAG_MAX, 2)), jnp.arange(TOK_DEV), side="right"))(jax.random.split(key_list[4], (N_DP * N_TABLE))).reshape((N_DP * N_TABLE, TOK_DEV)).astype(jnp.int32)
    hist_wix = plant(jax.random.randint(key_list[5], (HIST,), 0, NW), jax.random.fold_in(key_list[5], 1), 0, NW - 1).astype(jnp.int32)
    bag_weights = jnp.clip(jnp.exp(jax.random.uniform(key_list[6], (NW,), jnp.float32, math.log(0.099609375), math.log(1.0))), 0.099609375, 1.0).astype(jnp.bfloat16)
    item_owner_keys = jax.random.split(jax.random.fold_in(key_list[7], 1), BATCH // B_DEV)
    item_owner_turns = jax.random.permutation(jax.random.fold_in(key_list[7], 3), BATCH // B_DEV)
    item_owner = jax.vmap(lambda own, number: deal_out(jax.random.fold_in(key_list[7], 2), own, number, B_DEV, N_DP * N_TABLE, 1, CAP_ITEM, 1))(item_owner_keys, item_owner_turns).reshape((BATCH, 1))
    item_row = plant(jax.random.randint(key_list[8], (BATCH,), 0, ROWS_DEV), jax.random.fold_in(key_list[8], 1), 0, ROWS_DEV - 1).astype(jnp.int32)
    user_proj = bell_draw(key_list[9], (E, E), E ** -0.5, 0.375)
    item_proj = bell_draw(key_list[10], (E, E), E ** -0.5, 0.375)
    logit_scale = draw_logit_scale(jax.random.fold_in(key_list[12], 71), 0)
    return dict(user_table=user_table, item_table=item_table, hist_owner=hist_owner, hist_row=hist_row, hist_seg=hist_seg, hist_wix=hist_wix, bag_weights=bag_weights, item_owner=item_owner, item_row=item_row, user_proj=user_proj, item_proj=item_proj, logit_scale=logit_scale)


EPS = 1e-06

def tower(x, weight):
    u = jnp.dot(x, weight, preferred_element_type=jnp.float32)
    r = lax.rsqrt(lax.optimization_barrier(jnp.sum(u * u, -1, keepdims=True)) + EPS)
    return (u * r, r)

def reference(user_table, item_table, hist_owner, hist_row, hist_seg, hist_wix, bag_weights, item_owner, item_row, user_proj, item_proj, logit_scale):
    devices = N_DP * N_TABLE
    hist_id = (hist_owner[:, 0] * ROWS_DEV + hist_row).astype(jnp.int32)
    item_id = (item_owner[:, 0] * ROWS_DEV + item_row).astype(jnp.int32)
    seg = (hist_seg + (jnp.arange(devices, dtype=jnp.int32) * B_DEV)[:, None]).reshape(-1).astype(jnp.int32)
    wts = bag_weights[hist_wix].astype(jnp.float32)
    rows = user_table[hist_id].astype(jnp.float32)
    num = jax.ops.segment_sum(wts[:, None] * rows, seg, num_segments=BATCH)
    den = jax.ops.segment_sum(wts, seg, num_segments=BATCH)
    bag = (num / den[:, None]).astype(jnp.bfloat16)
    item_emb = item_table[item_id]
    un, ru = tower(bag, user_proj)
    vn, rv = tower(item_emb, item_proj)
    uh = un.astype(jnp.bfloat16)
    vh = vn.astype(jnp.bfloat16)
    scale = logit_scale[0]
    blk = min(512, BATCH)
    nblk = BATCH // blk
    cols = jnp.arange(BATCH, dtype=jnp.int32)

    def step(carry, inputs):
        ublock, index = inputs
        s = scale * jnp.dot(ublock, vh.T, preferred_element_type=jnp.float32)
        top = lax.optimization_barrier(jnp.max(s, -1, keepdims=True))
        expo = jnp.exp(s - top)
        prob = expo / lax.optimization_barrier(jnp.sum(expo, -1, keepdims=True))
        mine = index * blk + jnp.arange(blk, dtype=jnp.int32)
        hot = (cols[None, :] == mine[:, None]).astype(jnp.float32)
        pw = (prob - hot).astype(jnp.bfloat16)
        d_block = jnp.dot(pw, vh, preferred_element_type=jnp.float32)
        carry = carry + jnp.dot(pw.T, ublock, preferred_element_type=jnp.float32)
        return (carry, d_block)
    init = jnp.zeros((BATCH, E), jnp.float32)
    d_vsum, d_blocks = lax.scan(step, init, (uh.reshape(nblk, blk, E), jnp.arange(nblk, dtype=jnp.int32)))
    d_un = scale / BATCH * d_blocks.reshape(BATCH, E)
    d_vn = scale / BATCH * d_vsum
    d_u = ru * (d_un - un * lax.optimization_barrier(jnp.sum(un * d_un, -1, keepdims=True)))
    d_v = rv * (d_vn - vn * lax.optimization_barrier(jnp.sum(vn * d_vn, -1, keepdims=True)))
    hi = lax.Precision.HIGHEST
    user_proj_grad = jnp.dot(bag.astype(jnp.float32).T, d_u, precision=hi)
    item_proj_grad = jnp.dot(item_emb.astype(jnp.float32).T, d_v, precision=hi)
    d_bag = jnp.dot(d_u, user_proj.astype(jnp.float32).T, precision=hi)
    g_tok = (wts / den[seg])[:, None] * d_bag[seg]
    user_grad = jax.ops.segment_sum(g_tok, hist_id, num_segments=VOCAB)
    item_grad = jax.ops.segment_sum(d_v, item_id, num_segments=VOCAB)
    return (user_grad, item_grad, user_proj_grad, item_proj_grad)
```

```python
import jax
import jax.numpy as jnp
from jax import lax
from jax.sharding import PartitionSpec as P

EPS = 1e-06
AXES = ("dp", "table")


def tower(x, weight):
    u = jnp.dot(x, weight, preferred_element_type=jnp.float32)
    r = lax.rsqrt(jnp.sum(u * u, -1, keepdims=True) + EPS)
    return (u * r, r)


def slot_rank(owner, devices):
    onehot = (owner[:, None] == jnp.arange(devices, dtype=jnp.int32)[None, :]).astype(jnp.int32)
    before = jnp.cumsum(onehot, 0) - onehot
    return jnp.sum(before * onehot, 1)


def lookup(table, wanted):
    rows_dev = table.shape[0]
    valid = wanted < rows_dev
    picked = table[jnp.minimum(wanted, rows_dev - 1)]
    return jnp.where(valid[..., None], picked, jnp.zeros_like(picked))


def local(
    user_table,
    item_table,
    hist_owner,
    hist_row,
    hist_seg,
    hist_wix,
    bag_weights,
    item_owner,
    item_row,
    user_proj,
    item_proj,
    logit_scale,
):
    rows_dev, width = user_table.shape
    n_dp = lax.axis_size("dp")
    n_tab = lax.axis_size("table")
    devices = n_dp * n_tab
    tokens = hist_row.shape[0]
    samples = item_row.shape[0]
    cap = max(2, 2 * tokens // devices)
    cap_item = max(2, 2 * samples // devices)
    slots = cap + cap_item
    myself = lax.axis_index(AXES)
    user_owner = hist_owner[:, 0]
    goods_owner = item_owner[:, 0]
    user_slot = slot_rank(user_owner, devices)
    goods_slot = slot_rank(goods_owner, devices)
    user_key = user_owner * slots + user_slot
    goods_key = goods_owner * slots + cap + goods_slot
    keys = jnp.concatenate([user_key, goods_key])
    req = (
        jnp.full((devices * slots,), rows_dev, jnp.int32)
        .at[keys]
        .set(jnp.concatenate([hist_row, item_row]))
        .reshape(devices, slots)
    )
    want = lax.all_to_all(req, AXES, split_axis=0, concat_axis=0, tiled=True)
    user_want = want[:, :cap]
    goods_want = want[:, cap:]
    found = jnp.concatenate(
        [lookup(user_table, user_want), lookup(item_table, goods_want)], axis=1
    )
    back = lax.all_to_all(found, AXES, split_axis=0, concat_axis=0, tiled=True)
    got_rows = back.reshape(devices * slots, width)[keys]
    tok_rows = got_rows[:tokens]
    item_emb = got_rows[tokens:]
    entries = bag_weights.shape[0]
    wts = jnp.sum(
        jnp.where(
            hist_wix[:, None] == jnp.arange(entries, dtype=jnp.int32)[None, :],
            bag_weights[None, :].astype(jnp.float32),
            0.0,
        ),
        1,
    ).astype(jnp.bfloat16)
    segment = hist_seg[0]
    member = segment[None, :] == jnp.arange(samples, dtype=jnp.int32)[:, None]
    coef = jnp.where(member, wts[None, :], jnp.zeros((), jnp.bfloat16))
    numer = jnp.dot(coef, tok_rows, preferred_element_type=jnp.float32)
    denom = jnp.sum(coef.astype(jnp.float32), 1)
    bag = (numer / denom[:, None]).astype(jnp.bfloat16)
    un, ru = tower(bag, user_proj)
    vn, rv = tower(item_emb, item_proj)
    uh = un.astype(jnp.bfloat16)
    vh = vn.astype(jnp.bfloat16)
    scale = logit_scale[0]
    vh_all = lax.all_gather(vh, AXES, axis=0, tiled=True)
    uh_all = lax.all_gather(uh, AXES, axis=0, tiled=True)
    total = vh_all.shape[0]
    mine = myself * samples + jnp.arange(samples, dtype=jnp.int32)
    everyone = jnp.arange(total, dtype=jnp.int32)
    scores = scale * jnp.dot(uh, vh_all.T, preferred_element_type=jnp.float32)
    top = jnp.max(scores, -1)
    expo = jnp.exp(scores - top[:, None])
    norm = jnp.sum(expo, -1)
    stats_all = lax.all_gather(jnp.stack([top, norm], -1), AXES, axis=0, tiled=True)
    prob = expo / norm[:, None]
    hot = (everyone[None, :] == mine[:, None]).astype(jnp.float32)
    pw = (prob - hot).astype(jnp.bfloat16)
    d_un = scale / total * jnp.dot(pw, vh_all, preferred_element_type=jnp.float32)
    d_u = ru * (d_un - un * jnp.sum(un * d_un, -1, keepdims=True))
    highest = lax.Precision.HIGHEST
    user_part = jnp.dot(bag.astype(jnp.float32).T, d_u, precision=highest)
    d_bag = jnp.dot(d_u, user_proj.astype(jnp.float32).T, precision=highest)
    pick = jnp.concatenate([d_bag, denom[:, None]], axis=1)
    per_tok = jnp.dot(member.T.astype(jnp.float32), pick, precision=highest)
    g_tok = (wts.astype(jnp.float32) / per_tok[:, width])[:, None] * per_tok[:, :width]
    scores_c = scale * jnp.dot(vh, uh_all.T, preferred_element_type=jnp.float32)
    prob_c = jnp.exp(scores_c - stats_all[None, :, 0]) / stats_all[None, :, 1]
    hot_c = (everyone[None, :] == mine[:, None]).astype(jnp.float32)
    pw_c = (prob_c - hot_c).astype(jnp.bfloat16)
    d_vn = scale / total * jnp.dot(pw_c, uh_all, preferred_element_type=jnp.float32)
    d_v = rv * (d_vn - vn * jnp.sum(vn * d_vn, -1, keepdims=True))
    goods_part = jnp.dot(item_emb.astype(jnp.float32).T, d_v, precision=highest)
    user_proj_grad, item_proj_grad = lax.psum((user_part, goods_part), AXES)
    send = (
        jnp.zeros((devices * slots, width), jnp.float32)
        .at[keys]
        .set(jnp.concatenate([g_tok, d_v]))
        .reshape(devices, slots, width)
    )
    got = lax.all_to_all(send, AXES, split_axis=0, concat_axis=0, tiled=True)
    user_grad = (
        jnp.zeros((rows_dev, width), jnp.float32)
        .at[user_want.reshape(-1)]
        .add(got[:, :cap].reshape(-1, width), mode="drop")
    )
    item_grad = (
        jnp.zeros((rows_dev, width), jnp.float32)
        .at[goods_want.reshape(-1)]
        .add(got[:, cap:].reshape(-1, width), mode="drop")
    )
    return (user_grad, item_grad, user_proj_grad, item_proj_grad)


def solution(mesh):
    in_specs = (
        P(AXES, None),
        P(AXES, None),
        P(AXES, None),
        P(AXES),
        P(AXES, None),
        P(AXES),
        P(),
        P(AXES, None),
        P(AXES),
        P(),
        P(),
        P(),
    )
    out_specs = (P(AXES, None), P(AXES, None), P(), P())
    return jax.shard_map(local, mesh=mesh, in_specs=in_specs, out_specs=out_specs, check_vma=False)
```

```python
import jax
import jax.numpy as jnp
from jax import lax
from jax.sharding import PartitionSpec as P

EPS = 1e-06
AXES = ("dp", "table")


def tower(x, weight):
    u = jnp.dot(x, weight, preferred_element_type=jnp.float32)
    r = lax.rsqrt(jnp.sum(u * u, -1, keepdims=True) + EPS)
    return (u * r, r)


def slot_rank(owner, devices):
    onehot = (owner[:, None] == jnp.arange(devices, dtype=jnp.int32)[None, :]).astype(jnp.int32)
    before = jnp.cumsum(onehot, 0) - onehot
    return jnp.sum(before * onehot, 1)


def lookup(table, wanted):
    rows_dev = table.shape[0]
    valid = wanted < rows_dev
    picked = table[jnp.minimum(wanted, rows_dev - 1)]
    return jnp.where(valid[..., None], picked, jnp.zeros_like(picked))


def local(
    user_table,
    item_table,
    hist_owner,
    hist_row,
    hist_seg,
    hist_wix,
    bag_weights,
    item_owner,
    item_row,
    user_proj,
    item_proj,
    logit_scale,
):
    rows_dev, width = user_table.shape
    n_dp = lax.axis_size("dp")
    n_tab = lax.axis_size("table")
    devices = n_dp * n_tab
    tokens = hist_row.shape[0]
    samples = item_row.shape[0]
    cap = max(2, 2 * tokens // devices)
    cap_item = max(2, 2 * samples // devices)
    slots = cap + cap_item
    myself = lax.axis_index(AXES)
    user_owner = hist_owner[:, 0]
    goods_owner = item_owner[:, 0]
    user_slot = slot_rank(user_owner, devices)
    goods_slot = slot_rank(goods_owner, devices)
    user_key = user_owner * slots + user_slot
    goods_key = goods_owner * slots + cap + goods_slot
    keys = jnp.concatenate([user_key, goods_key])
    req = (
        jnp.full((devices * slots,), rows_dev, jnp.int32)
        .at[keys]
        .set(jnp.concatenate([hist_row, item_row]))
        .reshape(devices, slots)
    )
    want = lax.all_to_all(req, AXES, split_axis=0, concat_axis=0, tiled=True)
    user_want = want[:, :cap]
    goods_want = want[:, cap:]
    found = jnp.concatenate(
        [lookup(user_table, user_want), lookup(item_table, goods_want)], axis=1
    )
    back = lax.all_to_all(found, AXES, split_axis=0, concat_axis=0, tiled=True)
    got_rows = back.reshape(devices * slots, width)[keys]
    tok_rows = got_rows[:tokens]
    item_emb = got_rows[tokens:]
    entries = bag_weights.shape[0]
    wts = jnp.sum(
        jnp.where(
            hist_wix[:, None] == jnp.arange(entries, dtype=jnp.int32)[None, :],
            bag_weights[None, :].astype(jnp.float32),
            0.0,
        ),
        1,
    ).astype(jnp.bfloat16)
    segment = hist_seg[0]
    member = segment[None, :] == jnp.arange(samples, dtype=jnp.int32)[:, None]
    coef = jnp.where(member, wts[None, :], jnp.zeros((), jnp.bfloat16))
    numer = jnp.dot(coef, tok_rows, preferred_element_type=jnp.float32)
    denom = jnp.sum(coef.astype(jnp.float32), 1)
    bag = (numer / denom[:, None]).astype(jnp.bfloat16)
    un, ru = tower(bag, user_proj)
    vn, rv = tower(item_emb, item_proj)
    uh = un.astype(jnp.bfloat16)
    vh = vn.astype(jnp.bfloat16)
    scale = logit_scale[0]
    vh_all = lax.all_gather(vh, AXES, axis=0, tiled=True)
    uh_all = lax.all_gather(uh, AXES, axis=0, tiled=True)
    total = vh_all.shape[0]
    mine = myself * samples + jnp.arange(samples, dtype=jnp.int32)
    everyone = jnp.arange(total, dtype=jnp.int32)
    scores = scale * jnp.dot(uh, vh_all.T, preferred_element_type=jnp.float32)
    top = jnp.max(scores, -1)
    expo = jnp.exp(scores - top[:, None])
    norm = jnp.sum(expo, -1)
    stats = jnp.zeros((16, samples), jnp.float32).at[0].set(top).at[1].set(norm)
    stats_all = lax.all_gather(stats, AXES, axis=0, tiled=True).reshape(devices, 16, samples)
    top_all = stats_all[:, 0, :].reshape(total)
    norm_all = stats_all[:, 1, :].reshape(total)
    prob = expo / norm[:, None]
    hot = (everyone[None, :] == mine[:, None]).astype(jnp.float32)
    pw = (prob - hot).astype(jnp.bfloat16)
    d_un = scale / total * jnp.dot(pw, vh_all, preferred_element_type=jnp.float32)
    d_u = ru * (d_un - un * jnp.sum(un * d_un, -1, keepdims=True))
    highest = lax.Precision.HIGHEST
    user_part = jnp.dot(bag.astype(jnp.float32).T, d_u, precision=highest)
    d_bag = jnp.dot(d_u, user_proj.astype(jnp.float32).T, precision=highest)
    pick = jnp.concatenate([d_bag, denom[:, None]], axis=1)
    per_tok = jnp.dot(member.T.astype(jnp.float32), pick, precision=highest)
    g_tok = (wts.astype(jnp.float32) / per_tok[:, width])[:, None] * per_tok[:, :width]
    scores_c = scale * jnp.dot(vh, uh_all.T, preferred_element_type=jnp.float32)
    prob_c = jnp.exp(scores_c - top_all[None, :]) / norm_all[None, :]
    hot_c = (everyone[None, :] == mine[:, None]).astype(jnp.float32)
    pw_c = (prob_c - hot_c).astype(jnp.bfloat16)
    d_vn = scale / total * jnp.dot(pw_c, uh_all, preferred_element_type=jnp.float32)
    d_v = rv * (d_vn - vn * jnp.sum(vn * d_vn, -1, keepdims=True))
    goods_part = jnp.dot(item_emb.astype(jnp.float32).T, d_v, precision=highest)
    parts = jnp.stack([user_part, goods_part]).reshape(devices, -1, width)
    chunk = parts.shape[1]
    send = (
        jnp.zeros((devices * slots, width), jnp.float32)
        .at[keys]
        .set(jnp.concatenate([g_tok, d_v]))
        .reshape(devices, slots, width)
    )
    send = jnp.concatenate([send, parts], axis=1)
    got = lax.all_to_all(send, AXES, split_axis=0, concat_axis=0, tiled=True)
    reduced = jnp.sum(got[:, slots:], 0)
    padded = jnp.zeros((max(8, chunk), width), jnp.float32).at[:chunk].set(reduced)
    gathered = lax.all_gather(padded, AXES, axis=0, tiled=True).reshape(devices, -1, width)
    proj = gathered[:, :chunk].reshape(2, width, width)
    user_proj_grad = proj[0]
    item_proj_grad = proj[1]
    user_grad = (
        jnp.zeros((rows_dev, width), jnp.float32)
        .at[user_want.reshape(-1)]
        .add(got[:, :cap].reshape(-1, width), mode="drop")
    )
    item_grad = (
        jnp.zeros((rows_dev, width), jnp.float32)
        .at[goods_want.reshape(-1)]
        .add(got[:, cap:slots].reshape(-1, width), mode="drop")
    )
    return (user_grad, item_grad, user_proj_grad, item_proj_grad)


def solution(mesh):
    in_specs = (
        P(AXES, None),
        P(AXES, None),
        P(AXES, None),
        P(AXES),
        P(AXES, None),
        P(AXES),
        P(),
        P(AXES, None),
        P(AXES),
        P(),
        P(),
        P(),
    )
    out_specs = (P(AXES, None), P(AXES, None), P(), P())
    return jax.shard_map(local, mesh=mesh, in_specs=in_specs, out_specs=out_specs, check_vma=False)
```

```python
import jax
import jax.numpy as jnp
from jax import lax
from jax.sharding import PartitionSpec as P

EPS = 1e-06
AXES = ("dp", "table")


def tower(x, weight):
    u = jnp.dot(x, weight, preferred_element_type=jnp.float32)
    r = lax.rsqrt(jnp.sum(u * u, -1, keepdims=True) + EPS)
    return (u * r, r)


def slot_rank(owner, devices):
    onehot = (owner[:, None] == jnp.arange(devices, dtype=jnp.int32)[None, :]).astype(jnp.int32)
    before = jnp.cumsum(onehot, 0) - onehot
    return jnp.sum(before * onehot, 1)


def lookup(table, wanted):
    rows_dev = table.shape[0]
    valid = wanted < rows_dev
    picked = table[jnp.minimum(wanted, rows_dev - 1)]
    return jnp.where(valid[..., None], picked, jnp.zeros_like(picked))


def local(
    user_table,
    item_table,
    hist_owner,
    hist_row,
    hist_seg,
    hist_wix,
    bag_weights,
    item_owner,
    item_row,
    user_proj,
    item_proj,
    logit_scale,
):
    rows_dev, width = user_table.shape
    n_dp = lax.axis_size("dp")
    n_tab = lax.axis_size("table")
    devices = n_dp * n_tab
    tokens = hist_row.shape[0]
    samples = item_row.shape[0]
    cap = max(2, 2 * tokens // devices)
    cap_item = max(2, 2 * samples // devices)
    slots = cap + cap_item
    myself = lax.axis_index(AXES)
    user_owner = hist_owner[:, 0]
    goods_owner = item_owner[:, 0]
    user_slot = slot_rank(user_owner, devices)
    goods_slot = slot_rank(goods_owner, devices)
    user_key = user_owner * slots + user_slot
    goods_key = goods_owner * slots + cap + goods_slot
    keys = jnp.concatenate([user_key, goods_key])
    req = (
        jnp.full((devices * slots,), rows_dev, jnp.int32)
        .at[keys]
        .set(jnp.concatenate([hist_row, item_row]))
        .reshape(devices, slots)
    )
    want = lax.all_to_all(req, AXES, split_axis=0, concat_axis=0, tiled=True)
    user_want = want[:, :cap]
    goods_want = want[:, cap:]
    found = jnp.concatenate(
        [lookup(user_table, user_want), lookup(item_table, goods_want)], axis=1
    )
    back = lax.all_to_all(found, AXES, split_axis=0, concat_axis=0, tiled=True)
    got_rows = back.reshape(devices * slots, width)[keys]
    tok_rows = got_rows[:tokens]
    item_emb = got_rows[tokens:]
    entries = bag_weights.shape[0]
    wts = jnp.sum(
        jnp.where(
            hist_wix[:, None] == jnp.arange(entries, dtype=jnp.int32)[None, :],
            bag_weights[None, :].astype(jnp.float32),
            0.0,
        ),
        1,
    ).astype(jnp.bfloat16)
    segment = hist_seg[0]
    member = segment[None, :] == jnp.arange(samples, dtype=jnp.int32)[:, None]
    coef = jnp.where(member, wts[None, :], jnp.zeros((), jnp.bfloat16))
    numer = jnp.dot(coef, tok_rows, preferred_element_type=jnp.float32)
    denom = jnp.sum(coef.astype(jnp.float32), 1)
    bag = (numer / denom[:, None]).astype(jnp.bfloat16)
    un, ru = tower(bag, user_proj)
    vn, rv = tower(item_emb, item_proj)
    uh = un.astype(jnp.bfloat16)
    vh = vn.astype(jnp.bfloat16)
    scale = logit_scale[0]
    both = lax.all_gather(jnp.stack([uh, vh]), AXES, axis=1, tiled=True)
    uh_all = both[0]
    vh_all = both[1]
    total = vh_all.shape[0]
    mine = myself * samples + jnp.arange(samples, dtype=jnp.int32)
    everyone = jnp.arange(total, dtype=jnp.int32)
    scores = scale * jnp.dot(uh, vh_all.T, preferred_element_type=jnp.float32)
    top = jnp.max(scores, -1)
    expo = jnp.exp(scores - top[:, None])
    norm = jnp.sum(expo, -1)
    prob = expo / norm[:, None]
    hot = (everyone[None, :] == mine[:, None]).astype(jnp.float32)
    pw = (prob - hot).astype(jnp.bfloat16)
    d_un = scale / total * jnp.dot(pw, vh_all, preferred_element_type=jnp.float32)
    d_u = ru * (d_un - un * jnp.sum(un * d_un, -1, keepdims=True))
    highest = lax.Precision.HIGHEST
    user_part = jnp.dot(bag.astype(jnp.float32).T, d_u, precision=highest)
    d_bag = jnp.dot(d_u, user_proj.astype(jnp.float32).T, precision=highest)
    pick = jnp.concatenate([d_bag, denom[:, None]], axis=1)
    per_tok = jnp.dot(member.T.astype(jnp.float32), pick, precision=highest)
    g_tok = (wts.astype(jnp.float32) / per_tok[:, width])[:, None] * per_tok[:, :width]
    stats = jnp.concatenate([top, norm]).reshape(1, 1, -1)
    stats = jnp.broadcast_to(stats, (devices, 1, stats.shape[-1]))
    user_parts = user_part.reshape(devices, -1, width)
    stats = jnp.pad(stats, ((0, 0), (0, 0), (0, -stats.shape[-1] % width)))
    stats = stats.reshape(devices, -1, width)
    n_stat = stats.shape[1]
    got_s = lax.all_to_all(
        jnp.concatenate([stats, user_parts], axis=1), AXES, split_axis=0, concat_axis=0, tiled=True
    )
    flat_stats = got_s[:, :n_stat].reshape(devices, -1)
    top_all = flat_stats[:, :samples].reshape(total)
    norm_all = flat_stats[:, samples : 2 * samples].reshape(total)
    user_red = jnp.sum(got_s[:, n_stat:], 0)
    scores_c = scale * jnp.dot(vh, uh_all.T, preferred_element_type=jnp.float32)
    prob_c = jnp.exp(scores_c - top_all[None, :]) / norm_all[None, :]
    hot_c = (everyone[None, :] == mine[:, None]).astype(jnp.float32)
    pw_c = (prob_c - hot_c).astype(jnp.bfloat16)
    d_vn = scale / total * jnp.dot(pw_c, uh_all, preferred_element_type=jnp.float32)
    d_v = rv * (d_vn - vn * jnp.sum(vn * d_vn, -1, keepdims=True))
    goods_part = jnp.dot(item_emb.astype(jnp.float32).T, d_v, precision=highest)
    goods_parts = goods_part.reshape(devices, -1, width)
    chunk = goods_parts.shape[1]
    send = (
        jnp.zeros((devices * slots, width), jnp.float32)
        .at[keys]
        .set(jnp.concatenate([g_tok, d_v]))
        .reshape(devices, slots, width)
    )
    send = jnp.concatenate([send, goods_parts], axis=1)
    got = lax.all_to_all(send, AXES, split_axis=0, concat_axis=0, tiled=True)
    goods_red = jnp.sum(got[:, slots:], 0)
    red = jnp.concatenate([user_red, goods_red])
    padded = jnp.zeros((max(8, 2 * chunk), width), jnp.float32).at[: 2 * chunk].set(red)
    gathered = lax.all_gather(padded, AXES, axis=0, tiled=True).reshape(devices, -1, width)
    user_proj_grad = gathered[:, :chunk].reshape(width, width)
    item_proj_grad = gathered[:, chunk : 2 * chunk].reshape(width, width)
    user_grad = (
        jnp.zeros((rows_dev, width), jnp.float32)
        .at[user_want.reshape(-1)]
        .add(got[:, :cap].reshape(-1, width), mode="drop")
    )
    item_grad = (
        jnp.zeros((rows_dev, width), jnp.float32)
        .at[goods_want.reshape(-1)]
        .add(got[:, cap:slots].reshape(-1, width), mode="drop")
    )
    return (user_grad, item_grad, user_proj_grad, item_proj_grad)


def solution(mesh):
    in_specs = (
        P(AXES, None),
        P(AXES, None),
        P(AXES, None),
        P(AXES),
        P(AXES, None),
        P(AXES),
        P(),
        P(AXES, None),
        P(AXES),
        P(),
        P(),
        P(),
    )
    out_specs = (P(AXES, None), P(AXES, None), P(), P())
    return jax.shard_map(local, mesh=mesh, in_specs=in_specs, out_specs=out_specs, check_vma=False)
```

```python
import jax
import jax.numpy as jnp
from jax import lax
from jax.sharding import PartitionSpec as P

EPS = 1e-06
AXES = ("dp", "table")


def tower(x, weight):
    u = jnp.dot(x, weight, preferred_element_type=jnp.float32)
    r = lax.rsqrt(jnp.sum(u * u, -1, keepdims=True) + EPS)
    return (u * r, r)


def slot_rank(owner, devices):
    onehot = (owner[:, None] == jnp.arange(devices, dtype=jnp.int32)[None, :]).astype(jnp.int32)
    before = jnp.cumsum(onehot, 0) - onehot
    return jnp.sum(before * onehot, 1)


def lookup(table, wanted):
    rows_dev = table.shape[0]
    valid = wanted < rows_dev
    picked = table[jnp.minimum(wanted, rows_dev - 1)]
    return jnp.where(valid[..., None], picked, jnp.zeros_like(picked))


def local(
    user_table,
    item_table,
    hist_owner,
    hist_row,
    hist_seg,
    hist_wix,
    bag_weights,
    item_owner,
    item_row,
    user_proj,
    item_proj,
    logit_scale,
):
    rows_dev, width = user_table.shape
    n_dp = lax.axis_size("dp")
    n_tab = lax.axis_size("table")
    devices = n_dp * n_tab
    tokens = hist_row.shape[0]
    samples = item_row.shape[0]
    cap = max(2, 2 * tokens // devices)
    cap_item = max(2, 2 * samples // devices)
    slots = cap + cap_item
    myself = lax.axis_index(AXES)
    user_owner = hist_owner[:, 0]
    goods_owner = item_owner[:, 0]
    user_slot = slot_rank(user_owner, devices)
    goods_slot = slot_rank(goods_owner, devices)
    user_key = user_owner * slots + user_slot
    goods_key = goods_owner * slots + cap + goods_slot
    keys = jnp.concatenate([user_key, goods_key])
    entries = bag_weights.shape[0]
    segment = hist_seg[0]
    row_bits = max(1, (rows_dev - 1).bit_length())
    seg_bits = max(1, (samples - 1).bit_length())
    packed = jnp.concatenate(
        [
            hist_row | (segment << row_bits) | (hist_wix << (row_bits + seg_bits)),
            item_row | (jnp.arange(samples, dtype=jnp.int32) << row_bits),
        ]
    )
    info = jnp.full((devices * slots,), -1, jnp.int32).at[keys].set(packed)
    filled = info >= 0
    req = jnp.where(filled, info & ((1 << row_bits) - 1), rows_dev).reshape(devices, slots)
    slot_seg = (info >> row_bits) & ((1 << seg_bits) - 1)
    slot_wix = info >> (row_bits + seg_bits)
    is_user = (jnp.arange(devices * slots, dtype=jnp.int32) % slots) < cap
    want = lax.all_to_all(req, AXES, split_axis=0, concat_axis=0, tiled=True)
    user_want = want[:, :cap]
    goods_want = want[:, cap:]
    found = jnp.concatenate(
        [lookup(user_table, user_want), lookup(item_table, goods_want)], axis=1
    )
    back = lax.all_to_all(found, AXES, split_axis=0, concat_axis=0, tiled=True)
    back = back.reshape(devices * slots, width)
    wts = jnp.sum(
        jnp.where(
            slot_wix[:, None] == jnp.arange(entries, dtype=jnp.int32)[None, :],
            bag_weights[None, :].astype(jnp.float32),
            0.0,
        ),
        1,
    ).astype(jnp.bfloat16)
    sample_ids = jnp.arange(samples, dtype=jnp.int32)
    of_sample = filled[None, :] & (slot_seg[None, :] == sample_ids[:, None])
    member = of_sample & is_user[None, :]
    coef = jnp.where(member, wts[None, :], jnp.zeros((), jnp.bfloat16))
    numer = jnp.dot(coef, back, preferred_element_type=jnp.float32)
    denom = jnp.sum(coef.astype(jnp.float32), 1)
    bag = (numer / denom[:, None]).astype(jnp.bfloat16)
    item_pick = (of_sample & ~is_user[None, :]).astype(jnp.bfloat16)
    item_emb = jnp.dot(item_pick, back, preferred_element_type=jnp.float32).astype(jnp.bfloat16)
    un, ru = tower(bag, user_proj)
    vn, rv = tower(item_emb, item_proj)
    uh = un.astype(jnp.bfloat16)
    vh = vn.astype(jnp.bfloat16)
    scale = logit_scale[0]
    both = lax.all_gather(jnp.stack([uh, vh]), AXES, axis=1, tiled=True)
    uh_all = both[0]
    vh_all = both[1]
    total = vh_all.shape[0]
    mine = myself * samples + jnp.arange(samples, dtype=jnp.int32)
    everyone = jnp.arange(total, dtype=jnp.int32)
    scores = scale * jnp.dot(uh, vh_all.T, preferred_element_type=jnp.float32)
    top = jnp.max(scores, -1)
    expo = jnp.exp(scores - top[:, None])
    norm = jnp.sum(expo, -1)
    prob = expo / norm[:, None]
    hot = (everyone[None, :] == mine[:, None]).astype(jnp.float32)
    pw = (prob - hot).astype(jnp.bfloat16)
    d_un = scale / total * jnp.dot(pw, vh_all, preferred_element_type=jnp.float32)
    d_u = ru * (d_un - un * jnp.sum(un * d_un, -1, keepdims=True))
    highest = lax.Precision.HIGHEST
    user_part = jnp.dot(bag.astype(jnp.float32).T, d_u, precision=highest)
    d_bag = jnp.dot(d_u, user_proj.astype(jnp.float32).T, precision=highest)
    stats = jnp.concatenate([top, norm]).reshape(1, 1, -1)
    stats = jnp.broadcast_to(stats, (devices, 1, stats.shape[-1]))
    user_parts = user_part.reshape(devices, -1, width)
    stats = jnp.pad(stats, ((0, 0), (0, 0), (0, -stats.shape[-1] % width)))
    stats = stats.reshape(devices, -1, width)
    n_stat = stats.shape[1]
    got_s = lax.all_to_all(
        jnp.concatenate([stats, user_parts], axis=1), AXES, split_axis=0, concat_axis=0, tiled=True
    )
    flat_stats = got_s[:, :n_stat].reshape(devices, -1)
    top_all = flat_stats[:, :samples].reshape(total)
    norm_all = flat_stats[:, samples : 2 * samples].reshape(total)
    user_red = jnp.sum(got_s[:, n_stat:], 0)
    scores_c = scale * jnp.dot(vh, uh_all.T, preferred_element_type=jnp.float32)
    prob_c = jnp.exp(scores_c - top_all[None, :]) / norm_all[None, :]
    hot_c = (everyone[None, :] == mine[:, None]).astype(jnp.float32)
    pw_c = (prob_c - hot_c).astype(jnp.bfloat16)
    d_vn = scale / total * jnp.dot(pw_c, uh_all, preferred_element_type=jnp.float32)
    d_v = rv * (d_vn - vn * jnp.sum(vn * d_vn, -1, keepdims=True))
    goods_part = jnp.dot(item_emb.astype(jnp.float32).T, d_v, precision=highest)
    pick = jnp.concatenate([d_bag, d_v, denom[:, None]], axis=1)
    per_slot = jnp.dot(of_sample.T.astype(jnp.float32), pick, precision=highest)
    g_slot = (wts.astype(jnp.float32) / per_slot[:, 2 * width])[:, None] * per_slot[:, :width]
    g_slot = jnp.where(is_user[:, None], g_slot, per_slot[:, width : 2 * width])
    g_slot = jnp.where(filled[:, None], g_slot, 0.0)
    goods_parts = goods_part.reshape(devices, -1, width)
    chunk = goods_parts.shape[1]
    hi = goods_parts.astype(jnp.bfloat16)
    lo = (goods_parts - hi.astype(jnp.float32)).astype(jnp.bfloat16)
    send = jnp.concatenate(
        [g_slot.astype(jnp.bfloat16).reshape(devices, slots, width), hi, lo], axis=1
    )
    got = lax.all_to_all(send, AXES, split_axis=0, concat_axis=0, tiled=True)
    tail = got[:, slots:].astype(jnp.float32)
    goods_red = jnp.sum(tail[:, :chunk] + tail[:, chunk:], 0)
    red = jnp.concatenate([user_red, goods_red])
    padded = jnp.zeros((max(8, 2 * chunk), width), jnp.float32).at[: 2 * chunk].set(red)
    gathered = lax.all_gather(padded, AXES, axis=0, tiled=True).reshape(devices, -1, width)
    user_proj_grad = gathered[:, :chunk].reshape(width, width)
    item_proj_grad = gathered[:, chunk : 2 * chunk].reshape(width, width)
    user_grad = (
        jnp.zeros((rows_dev, width), jnp.float32)
        .at[user_want.reshape(-1)]
        .add(got[:, :cap].reshape(-1, width).astype(jnp.float32), mode="drop")
    )
    item_grad = (
        jnp.zeros((rows_dev, width), jnp.float32)
        .at[goods_want.reshape(-1)]
        .add(got[:, cap:slots].reshape(-1, width).astype(jnp.float32), mode="drop")
    )
    return (user_grad, item_grad, user_proj_grad, item_proj_grad)


def solution(mesh):
    in_specs = (
        P(AXES, None),
        P(AXES, None),
        P(AXES, None),
        P(AXES),
        P(AXES, None),
        P(AXES),
        P(),
        P(AXES, None),
        P(AXES),
        P(),
        P(),
        P(),
    )
    out_specs = (P(AXES, None), P(AXES, None), P(), P())
    return jax.shard_map(local, mesh=mesh, in_specs=in_specs, out_specs=out_specs, check_vma=False)
```

```python
import jax
import jax.numpy as jnp
from jax import lax
from jax.sharding import PartitionSpec as P

EPS = 1e-06
AXES = ("dp", "table")


def tower(x, weight):
    u = jnp.dot(x, weight, preferred_element_type=jnp.float32)
    r = lax.rsqrt(jnp.sum(u * u, -1, keepdims=True) + EPS)
    return (u * r, r)


def slot_rank(owner, devices):
    onehot = (owner[:, None] == jnp.arange(devices, dtype=jnp.int32)[None, :]).astype(jnp.int32)
    before = jnp.cumsum(onehot, 0) - onehot
    return jnp.sum(before * onehot, 1)


def lookup(table, wanted):
    rows_dev = table.shape[0]
    valid = wanted < rows_dev
    picked = table[jnp.minimum(wanted, rows_dev - 1)]
    return jnp.where(valid[..., None], picked, jnp.zeros_like(picked))


def exchange(x):
    return lax.all_to_all(x, AXES, split_axis=1, concat_axis=1, tiled=True)


def local(
    user_table,
    item_table,
    hist_owner,
    hist_row,
    hist_seg,
    hist_wix,
    bag_weights,
    item_owner,
    item_row,
    user_proj,
    item_proj,
    logit_scale,
):
    rows_dev, width = user_table.shape
    n_dp = lax.axis_size("dp")
    n_tab = lax.axis_size("table")
    devices = n_dp * n_tab
    tokens = hist_row.shape[0]
    samples = item_row.shape[0]
    cap = max(2, 2 * tokens // devices)
    cap_item = max(2, 2 * samples // devices)
    slots = cap + cap_item
    myself = lax.axis_index(AXES)
    entries = bag_weights.shape[0]
    segment = hist_seg[0]
    sample_ids = jnp.arange(samples, dtype=jnp.int32)
    owner = jnp.concatenate([hist_owner[:, 0], item_owner[:, 0]])
    rank = jnp.concatenate(
        [slot_rank(hist_owner[:, 0], devices), cap + slot_rank(item_owner[:, 0], devices)]
    )
    row = jnp.concatenate([hist_row, item_row])
    fields = jnp.stack(
        [
            row & 255,
            row >> 8,
            jnp.concatenate([segment, sample_ids]),
            jnp.concatenate([hist_wix, jnp.zeros((samples,), jnp.int32)]),
            jnp.ones_like(row),
        ]
    )
    by_owner = (owner[None, :] == jnp.arange(devices, dtype=jnp.int32)[:, None]).astype(jnp.bfloat16)
    planes = (fields.astype(jnp.bfloat16)[:, None, :] * by_owner[None, :, :]).reshape(-1, owner.shape[0])
    by_rank = (rank[:, None] == jnp.arange(slots, dtype=jnp.int32)[None, :]).astype(jnp.bfloat16)
    table = jnp.dot(planes, by_rank, preferred_element_type=jnp.float32)
    table = table.astype(jnp.int32).reshape(fields.shape[0], devices, slots)
    table = jnp.transpose(table, (0, 2, 1)).reshape(fields.shape[0], slots * devices)
    slot_row = table[0] + 256 * table[1]
    slot_seg = table[2]
    slot_wix = table[3]
    filled = table[4] > 0
    req = jnp.where(filled, slot_row, rows_dev).reshape(slots, devices)
    is_user = jnp.arange(slots * devices, dtype=jnp.int32) < cap * devices
    want = exchange(req)
    user_want = want[:cap]
    goods_want = want[cap:]
    found = jnp.concatenate(
        [lookup(user_table, user_want), lookup(item_table, goods_want)], axis=0
    )
    back = exchange(found).reshape(slots * devices, width)
    wts = jnp.sum(
        jnp.where(
            slot_wix[:, None] == jnp.arange(entries, dtype=jnp.int32)[None, :],
            bag_weights[None, :].astype(jnp.float32),
            0.0,
        ),
        1,
    ).astype(jnp.bfloat16)
    of_sample = filled[None, :] & (slot_seg[None, :] == sample_ids[:, None])
    member = of_sample & is_user[None, :]
    coef = jnp.where(member, wts[None, :], jnp.zeros((), jnp.bfloat16))
    numer = jnp.dot(coef, back, preferred_element_type=jnp.float32)
    denom = jnp.sum(coef.astype(jnp.float32), 1)
    bag = (numer / denom[:, None]).astype(jnp.bfloat16)
    item_pick = (of_sample & ~is_user[None, :]).astype(jnp.bfloat16)
    item_emb = jnp.dot(item_pick, back, preferred_element_type=jnp.float32).astype(jnp.bfloat16)
    un, ru = tower(bag, user_proj)
    vn, rv = tower(item_emb, item_proj)
    uh = un.astype(jnp.bfloat16)
    vh = vn.astype(jnp.bfloat16)
    scale = logit_scale[0]
    both = lax.all_gather(jnp.stack([uh, vh]), AXES, axis=1, tiled=True)
    uh_all = both[0]
    vh_all = both[1]
    total = vh_all.shape[0]
    mine = myself * samples + sample_ids
    everyone = jnp.arange(total, dtype=jnp.int32)
    scores = scale * jnp.dot(uh, vh_all.T, preferred_element_type=jnp.float32)
    top = jnp.max(scores, -1)
    expo = jnp.exp(scores - top[:, None])
    norm = jnp.sum(expo, -1)
    prob = expo / norm[:, None]
    hot = (everyone[None, :] == mine[:, None]).astype(jnp.float32)
    pw = (prob - hot).astype(jnp.bfloat16)
    d_un = scale / total * jnp.dot(pw, vh_all, preferred_element_type=jnp.float32)
    d_u = ru * (d_un - un * jnp.sum(un * d_un, -1, keepdims=True))
    highest = lax.Precision.HIGHEST
    user_part = jnp.dot(bag.astype(jnp.float32).T, d_u, precision=highest)
    d_bag = jnp.dot(d_u, user_proj.astype(jnp.float32).T, precision=highest)
    stats = jnp.concatenate([top, norm]).reshape(1, 1, -1)
    stats = jnp.broadcast_to(stats, (devices, 1, stats.shape[-1]))
    stats = jnp.pad(stats, ((0, 0), (0, 0), (0, -stats.shape[-1] % width)))
    stats = stats.reshape(devices, -1, width)
    user_parts = user_part.reshape(devices, -1, width)
    n_stat = stats.shape[1]
    got_s = lax.all_to_all(
        jnp.concatenate([stats, user_parts], axis=1), AXES, split_axis=0, concat_axis=0, tiled=True
    )
    flat_stats = got_s[:, :n_stat].reshape(devices, -1)
    top_all = flat_stats[:, :samples].reshape(total)
    norm_all = flat_stats[:, samples : 2 * samples].reshape(total)
    user_red = jnp.sum(got_s[:, n_stat:], 0)
    scores_c = scale * jnp.dot(vh, uh_all.T, preferred_element_type=jnp.float32)
    prob_c = jnp.exp(scores_c - top_all[None, :]) / norm_all[None, :]
    hot_c = (everyone[None, :] == mine[:, None]).astype(jnp.float32)
    pw_c = (prob_c - hot_c).astype(jnp.bfloat16)
    d_vn = scale / total * jnp.dot(pw_c, uh_all, preferred_element_type=jnp.float32)
    d_v = rv * (d_vn - vn * jnp.sum(vn * d_vn, -1, keepdims=True))
    goods_part = jnp.dot(item_emb.astype(jnp.float32).T, d_v, precision=highest)
    pick = jnp.concatenate([d_bag, d_v, denom[:, None]], axis=1)
    per_slot = jnp.dot(of_sample.T.astype(jnp.float32), pick, precision=highest)
    g_slot = (wts.astype(jnp.float32) / per_slot[:, 2 * width])[:, None] * per_slot[:, :width]
    g_slot = jnp.where(is_user[:, None], g_slot, per_slot[:, width : 2 * width])
    g_slot = jnp.where(filled[:, None], g_slot, 0.0)
    goods_parts = jnp.transpose(goods_part.reshape(devices, -1, width), (1, 0, 2))
    chunk = goods_parts.shape[0]
    hi = goods_parts.astype(jnp.bfloat16)
    lo = (goods_parts - hi.astype(jnp.float32)).astype(jnp.bfloat16)
    send = jnp.concatenate(
        [g_slot.astype(jnp.bfloat16).reshape(slots, devices, width), hi, lo], axis=0
    )
    got = exchange(send)
    tail = got[slots:].astype(jnp.float32)
    goods_red = jnp.sum(tail[:chunk] + tail[chunk:], 1)
    red = jnp.concatenate([user_red, goods_red])
    spread = lax.all_to_all(
        jnp.broadcast_to(red[None], (devices,) + red.shape), AXES, split_axis=0, concat_axis=0, tiled=True
    )
    user_proj_grad = spread[:, :chunk].reshape(width, width)
    item_proj_grad = spread[:, chunk:].reshape(width, width)
    user_grad = (
        jnp.zeros((rows_dev, width), jnp.float32)
        .at[user_want.reshape(-1)]
        .add(got[:cap].reshape(-1, width).astype(jnp.float32), mode="drop")
    )
    item_grad = (
        jnp.zeros((rows_dev, width), jnp.float32)
        .at[goods_want.reshape(-1)]
        .add(got[cap:slots].reshape(-1, width).astype(jnp.float32), mode="drop")
    )
    return (user_grad, item_grad, user_proj_grad, item_proj_grad)


def solution(mesh):
    in_specs = (
        P(AXES, None),
        P(AXES, None),
        P(AXES, None),
        P(AXES),
        P(AXES, None),
        P(AXES),
        P(),
        P(AXES, None),
        P(AXES),
        P(),
        P(),
        P(),
    )
    out_specs = (P(AXES, None), P(AXES, None), P(), P())
    return jax.shard_map(local, mesh=mesh, in_specs=in_specs, out_specs=out_specs, check_vma=False)
```

```python
import jax
import jax.numpy as jnp
from jax import lax
from jax.sharding import PartitionSpec as P

EPS = 1e-06
AXES = ("dp", "table")


def tower(x, weight):
    u = jnp.dot(x, weight, preferred_element_type=jnp.float32)
    r = lax.rsqrt(jnp.sum(u * u, -1, keepdims=True) + EPS)
    return (u * r, r)


def slot_rank(owner, devices):
    onehot = (owner[:, None] == jnp.arange(devices, dtype=jnp.int32)[None, :]).astype(jnp.int32)
    before = jnp.cumsum(onehot, 0) - onehot
    return jnp.sum(before * onehot, 1)


def pick_rows(table, wanted):
    rows_dev = table.shape[0]
    flat = wanted.reshape(-1)
    onehot = (flat[:, None] == jnp.arange(rows_dev, dtype=jnp.int32)[None, :]).astype(table.dtype)
    picked = jnp.dot(onehot, table, preferred_element_type=jnp.float32).astype(table.dtype)
    return picked.reshape(wanted.shape + table.shape[1:])


def add_rows(rows_dev, wanted, values):
    flat = wanted.reshape(-1)
    onehot = (jnp.arange(rows_dev, dtype=jnp.int32)[:, None] == flat[None, :]).astype(values.dtype)
    return jnp.dot(onehot, values.reshape(flat.shape[0], -1), preferred_element_type=jnp.float32)


def exchange(x):
    return lax.all_to_all(x, AXES, split_axis=1, concat_axis=1, tiled=True)


def local(
    user_table,
    item_table,
    hist_owner,
    hist_row,
    hist_seg,
    hist_wix,
    bag_weights,
    item_owner,
    item_row,
    user_proj,
    item_proj,
    logit_scale,
):
    rows_dev, width = user_table.shape
    n_dp = lax.axis_size("dp")
    n_tab = lax.axis_size("table")
    devices = n_dp * n_tab
    tokens = hist_row.shape[0]
    samples = item_row.shape[0]
    cap = max(2, 2 * tokens // devices)
    cap_item = max(2, 2 * samples // devices)
    slots = cap + cap_item
    myself = lax.axis_index(AXES)
    entries = bag_weights.shape[0]
    segment = hist_seg[0]
    sample_ids = jnp.arange(samples, dtype=jnp.int32)
    owner = jnp.concatenate([hist_owner[:, 0], item_owner[:, 0]])
    rank = jnp.concatenate(
        [slot_rank(hist_owner[:, 0], devices), cap + slot_rank(item_owner[:, 0], devices)]
    )
    row = jnp.concatenate([hist_row, item_row])
    fields = jnp.stack(
        [
            row & 255,
            row >> 8,
            jnp.concatenate([segment, sample_ids]),
            jnp.concatenate([hist_wix, jnp.zeros((samples,), jnp.int32)]),
            jnp.ones_like(row),
        ]
    )
    by_owner = (owner[None, :] == jnp.arange(devices, dtype=jnp.int32)[:, None]).astype(jnp.bfloat16)
    planes = (fields.astype(jnp.bfloat16)[:, None, :] * by_owner[None, :, :]).reshape(-1, owner.shape[0])
    by_rank = (rank[:, None] == jnp.arange(slots, dtype=jnp.int32)[None, :]).astype(jnp.bfloat16)
    table = jnp.dot(planes, by_rank, preferred_element_type=jnp.float32)
    table = table.astype(jnp.int32).reshape(fields.shape[0], devices, slots)
    table = jnp.transpose(table, (0, 2, 1)).reshape(fields.shape[0], slots * devices)
    slot_row = table[0] + 256 * table[1]
    slot_seg = table[2]
    slot_wix = table[3]
    filled = table[4] > 0
    req = jnp.where(filled, slot_row, rows_dev).reshape(slots, devices)
    is_user = jnp.arange(slots * devices, dtype=jnp.int32) < cap * devices
    want = exchange(req)
    user_want = want[:cap]
    goods_want = want[cap:]
    found = jnp.concatenate(
        [pick_rows(user_table, user_want), pick_rows(item_table, goods_want)], axis=0
    )
    back = exchange(found).reshape(slots * devices, width)
    wts = jnp.sum(
        jnp.where(
            slot_wix[:, None] == jnp.arange(entries, dtype=jnp.int32)[None, :],
            bag_weights[None, :].astype(jnp.float32),
            0.0,
        ),
        1,
    ).astype(jnp.bfloat16)
    of_sample = filled[None, :] & (slot_seg[None, :] == sample_ids[:, None])
    member = of_sample & is_user[None, :]
    coef = jnp.where(member, wts[None, :], jnp.zeros((), jnp.bfloat16))
    numer = jnp.dot(coef, back, preferred_element_type=jnp.float32)
    denom = jnp.sum(coef.astype(jnp.float32), 1)
    bag = (numer / denom[:, None]).astype(jnp.bfloat16)
    item_pick = (of_sample & ~is_user[None, :]).astype(jnp.bfloat16)
    item_emb = jnp.dot(item_pick, back, preferred_element_type=jnp.float32).astype(jnp.bfloat16)
    un, ru = tower(bag, user_proj)
    vn, rv = tower(item_emb, item_proj)
    uh = un.astype(jnp.bfloat16)
    vh = vn.astype(jnp.bfloat16)
    scale = logit_scale[0]
    both = lax.all_gather(jnp.stack([uh, vh]), AXES, axis=1, tiled=True)
    uh_all = both[0]
    vh_all = both[1]
    total = vh_all.shape[0]
    mine = myself * samples + sample_ids
    everyone = jnp.arange(total, dtype=jnp.int32)
    scores = scale * jnp.dot(uh, vh_all.T, preferred_element_type=jnp.float32)
    top = jnp.max(scores, -1)
    expo = jnp.exp(scores - top[:, None])
    norm = jnp.sum(expo, -1)
    prob = expo / norm[:, None]
    hot = (everyone[None, :] == mine[:, None]).astype(jnp.float32)
    pw = (prob - hot).astype(jnp.bfloat16)
    d_un = scale / total * jnp.dot(pw, vh_all, preferred_element_type=jnp.float32)
    d_u = ru * (d_un - un * jnp.sum(un * d_un, -1, keepdims=True))
    highest = lax.Precision.HIGHEST
    user_part = jnp.dot(bag.astype(jnp.float32).T, d_u, precision=highest)
    d_bag = jnp.dot(d_u, user_proj.astype(jnp.float32).T, precision=highest)
    stats = jnp.concatenate([top, norm]).reshape(1, 1, -1)
    stats = jnp.broadcast_to(stats, (devices, 1, stats.shape[-1]))
    stats = jnp.pad(stats, ((0, 0), (0, 0), (0, -stats.shape[-1] % width)))
    stats = stats.reshape(devices, -1, width)
    user_parts = user_part.reshape(devices, -1, width)
    n_stat = stats.shape[1]
    got_s = lax.all_to_all(
        jnp.concatenate([stats, user_parts], axis=1), AXES, split_axis=0, concat_axis=0, tiled=True
    )
    flat_stats = got_s[:, :n_stat].reshape(devices, -1)
    top_all = flat_stats[:, :samples].reshape(total)
    norm_all = flat_stats[:, samples : 2 * samples].reshape(total)
    user_red = jnp.sum(got_s[:, n_stat:], 0)
    scores_c = scale * jnp.dot(vh, uh_all.T, preferred_element_type=jnp.float32)
    prob_c = jnp.exp(scores_c - top_all[None, :]) / norm_all[None, :]
    hot_c = (everyone[None, :] == mine[:, None]).astype(jnp.float32)
    pw_c = (prob_c - hot_c).astype(jnp.bfloat16)
    d_vn = scale / total * jnp.dot(pw_c, uh_all, preferred_element_type=jnp.float32)
    d_v = rv * (d_vn - vn * jnp.sum(vn * d_vn, -1, keepdims=True))
    goods_part = jnp.dot(item_emb.astype(jnp.float32).T, d_v, precision=highest)
    pick = jnp.concatenate([d_bag, d_v, denom[:, None]], axis=1)
    per_slot = jnp.dot(of_sample.T.astype(jnp.float32), pick, precision=highest)
    g_slot = (wts.astype(jnp.float32) / per_slot[:, 2 * width])[:, None] * per_slot[:, :width]
    g_slot = jnp.where(is_user[:, None], g_slot, per_slot[:, width : 2 * width])
    g_slot = jnp.where(filled[:, None], g_slot, 0.0)
    goods_parts = jnp.transpose(goods_part.reshape(devices, -1, width), (1, 0, 2))
    chunk = goods_parts.shape[0]
    hi = goods_parts.astype(jnp.bfloat16)
    lo = (goods_parts - hi.astype(jnp.float32)).astype(jnp.bfloat16)
    send = jnp.concatenate(
        [g_slot.astype(jnp.bfloat16).reshape(slots, devices, width), hi, lo], axis=0
    )
    got = exchange(send)
    tail = got[slots:].astype(jnp.float32)
    goods_red = jnp.sum(tail[:chunk] + tail[chunk:], 1)
    red = jnp.concatenate([user_red, goods_red])
    spread = lax.all_to_all(
        jnp.broadcast_to(red[None], (devices,) + red.shape), AXES, split_axis=0, concat_axis=0, tiled=True
    )
    user_proj_grad = spread[:, :chunk].reshape(width, width)
    item_proj_grad = spread[:, chunk:].reshape(width, width)
    user_grad = add_rows(rows_dev, user_want, got[:cap])
    item_grad = add_rows(rows_dev, goods_want, got[cap:slots])
    return (user_grad, item_grad, user_proj_grad, item_proj_grad)


def solution(mesh):
    in_specs = (
        P(AXES, None),
        P(AXES, None),
        P(AXES, None),
        P(AXES),
        P(AXES, None),
        P(AXES),
        P(),
        P(AXES, None),
        P(AXES),
        P(),
        P(),
        P(),
    )
    out_specs = (P(AXES, None), P(AXES, None), P(), P())
    return jax.shard_map(local, mesh=mesh, in_specs=in_specs, out_specs=out_specs, check_vma=False)
```

```python
import jax
import jax.numpy as jnp
from jax import lax
from jax.sharding import PartitionSpec as P

EPS = 1e-06
AXES = ("dp", "table")


def tower(x, weight):
    u = jnp.dot(x, weight, preferred_element_type=jnp.float32)
    r = lax.rsqrt(jnp.sum(u * u, -1, keepdims=True) + EPS)
    return (u * r, r)


def slot_rank(owner, devices):
    onehot = (owner[:, None] == jnp.arange(devices, dtype=jnp.int32)[None, :]).astype(jnp.int32)
    before = jnp.cumsum(onehot, 0) - onehot
    return jnp.sum(before * onehot, 1)


def pick_rows(table, wanted):
    rows_dev = table.shape[0]
    flat = wanted.reshape(-1)
    onehot = (flat[:, None] == jnp.arange(rows_dev, dtype=jnp.int32)[None, :]).astype(table.dtype)
    picked = jnp.dot(onehot, table, preferred_element_type=jnp.float32).astype(table.dtype)
    return picked.reshape(wanted.shape + table.shape[1:])


def add_rows(rows_dev, wanted, values):
    flat = wanted.reshape(-1)
    onehot = (jnp.arange(rows_dev, dtype=jnp.int32)[:, None] == flat[None, :]).astype(values.dtype)
    return jnp.dot(onehot, values.reshape(flat.shape[0], -1), preferred_element_type=jnp.float32)


def exchange(x):
    return lax.all_to_all(x, AXES, split_axis=1, concat_axis=1, tiled=True)


def local(
    user_table,
    item_table,
    hist_owner,
    hist_row,
    hist_seg,
    hist_wix,
    bag_weights,
    item_owner,
    item_row,
    user_proj,
    item_proj,
    logit_scale,
):
    rows_dev, width = user_table.shape
    n_dp = lax.axis_size("dp")
    n_tab = lax.axis_size("table")
    devices = n_dp * n_tab
    tokens = hist_row.shape[0]
    samples = item_row.shape[0]
    cap = max(2, 2 * tokens // devices)
    cap_item = max(2, 2 * samples // devices)
    slots = cap + cap_item
    myself = lax.axis_index(AXES)
    entries = bag_weights.shape[0]
    segment = hist_seg[0]
    sample_ids = jnp.arange(samples, dtype=jnp.int32)
    owner = jnp.concatenate([hist_owner[:, 0], item_owner[:, 0]])
    rank = jnp.concatenate(
        [slot_rank(hist_owner[:, 0], devices), cap + slot_rank(item_owner[:, 0], devices)]
    )
    row = jnp.concatenate([hist_row, item_row])
    fields = jnp.stack(
        [
            row & 255,
            row >> 8,
            jnp.concatenate([segment, sample_ids]),
            jnp.concatenate([hist_wix, jnp.zeros((samples,), jnp.int32)]),
            jnp.ones_like(row),
        ]
    )
    by_owner = (owner[None, :] == jnp.arange(devices, dtype=jnp.int32)[:, None]).astype(jnp.bfloat16)
    planes = (fields.astype(jnp.bfloat16)[:, None, :] * by_owner[None, :, :]).reshape(-1, owner.shape[0])
    by_rank = (rank[:, None] == jnp.arange(slots, dtype=jnp.int32)[None, :]).astype(jnp.bfloat16)
    table = jnp.dot(planes, by_rank, preferred_element_type=jnp.float32)
    table = table.astype(jnp.int32).reshape(fields.shape[0], devices, slots)
    table = jnp.transpose(table, (0, 2, 1)).reshape(fields.shape[0], slots * devices)
    slot_row = table[0] + 256 * table[1]
    slot_seg = table[2]
    slot_wix = table[3]
    filled = table[4] > 0
    req = jnp.where(filled, slot_row, rows_dev).reshape(slots, devices)
    is_user = jnp.arange(slots * devices, dtype=jnp.int32) < cap * devices
    want = exchange(req)
    user_want = want[:cap]
    goods_want = want[cap:]
    goods_back = exchange(pick_rows(item_table, goods_want))
    user_back = exchange(pick_rows(user_table, user_want))
    wts = jnp.sum(
        jnp.where(
            slot_wix[:, None] == jnp.arange(entries, dtype=jnp.int32)[None, :],
            bag_weights[None, :].astype(jnp.float32),
            0.0,
        ),
        1,
    ).astype(jnp.bfloat16)
    of_sample = filled[None, :] & (slot_seg[None, :] == sample_ids[:, None])
    item_pick = of_sample[:, cap * devices :].astype(jnp.bfloat16)
    item_emb = jnp.dot(
        item_pick, goods_back.reshape(-1, width), preferred_element_type=jnp.float32
    ).astype(jnp.bfloat16)
    vn, rv = tower(item_emb, item_proj)
    vh = vn.astype(jnp.bfloat16)
    vh_all = lax.all_gather(vh, AXES, axis=0, tiled=True)
    coef = jnp.where(of_sample[:, : cap * devices], wts[None, : cap * devices], jnp.zeros((), jnp.bfloat16))
    numer = jnp.dot(coef, user_back.reshape(-1, width), preferred_element_type=jnp.float32)
    denom = jnp.sum(coef.astype(jnp.float32), 1)
    bag = (numer / denom[:, None]).astype(jnp.bfloat16)
    un, ru = tower(bag, user_proj)
    uh = un.astype(jnp.bfloat16)
    uh_all = lax.all_gather(uh, AXES, axis=0, tiled=True)
    scale = logit_scale[0]
    total = vh_all.shape[0]
    mine = myself * samples + sample_ids
    everyone = jnp.arange(total, dtype=jnp.int32)
    scores = scale * jnp.dot(uh, vh_all.T, preferred_element_type=jnp.float32)
    top = jnp.max(scores, -1)
    expo = jnp.exp(scores - top[:, None])
    norm = jnp.sum(expo, -1)
    prob = expo / norm[:, None]
    hot = (everyone[None, :] == mine[:, None]).astype(jnp.float32)
    pw = (prob - hot).astype(jnp.bfloat16)
    d_un = scale / total * jnp.dot(pw, vh_all, preferred_element_type=jnp.float32)
    d_u = ru * (d_un - un * jnp.sum(un * d_un, -1, keepdims=True))
    highest = lax.Precision.HIGHEST
    user_part = jnp.dot(bag.astype(jnp.float32).T, d_u, precision=highest)
    d_bag = jnp.dot(d_u, user_proj.astype(jnp.float32).T, precision=highest)
    stats = jnp.concatenate([top, norm]).reshape(1, 1, -1)
    stats = jnp.broadcast_to(stats, (devices, 1, stats.shape[-1]))
    stats = jnp.pad(stats, ((0, 0), (0, 0), (0, -stats.shape[-1] % width)))
    stats = stats.reshape(devices, -1, width)
    user_parts = user_part.reshape(devices, -1, width)
    n_stat = stats.shape[1]
    got_s = lax.all_to_all(
        jnp.concatenate([stats, user_parts], axis=1), AXES, split_axis=0, concat_axis=0, tiled=True
    )
    flat_stats = got_s[:, :n_stat].reshape(devices, -1)
    top_all = flat_stats[:, :samples].reshape(total)
    norm_all = flat_stats[:, samples : 2 * samples].reshape(total)
    user_red = jnp.sum(got_s[:, n_stat:], 0)
    scores_c = scale * jnp.dot(vh, uh_all.T, preferred_element_type=jnp.float32)
    prob_c = jnp.exp(scores_c - top_all[None, :]) / norm_all[None, :]
    hot_c = (everyone[None, :] == mine[:, None]).astype(jnp.float32)
    pw_c = (prob_c - hot_c).astype(jnp.bfloat16)
    d_vn = scale / total * jnp.dot(pw_c, uh_all, preferred_element_type=jnp.float32)
    d_v = rv * (d_vn - vn * jnp.sum(vn * d_vn, -1, keepdims=True))
    goods_part = jnp.dot(item_emb.astype(jnp.float32).T, d_v, precision=highest)
    pick = jnp.concatenate([d_bag, d_v, denom[:, None]], axis=1)
    per_slot = jnp.dot(of_sample.T.astype(jnp.float32), pick, precision=highest)
    g_slot = (wts.astype(jnp.float32) / per_slot[:, 2 * width])[:, None] * per_slot[:, :width]
    g_slot = jnp.where(is_user[:, None], g_slot, per_slot[:, width : 2 * width])
    g_slot = jnp.where(filled[:, None], g_slot, 0.0)
    goods_parts = jnp.transpose(goods_part.reshape(devices, -1, width), (1, 0, 2))
    chunk = goods_parts.shape[0]
    hi = goods_parts.astype(jnp.bfloat16)
    lo = (goods_parts - hi.astype(jnp.float32)).astype(jnp.bfloat16)
    send = jnp.concatenate(
        [g_slot.astype(jnp.bfloat16).reshape(slots, devices, width), hi, lo], axis=0
    )
    got = exchange(send)
    tail = got[slots:].astype(jnp.float32)
    goods_red = jnp.sum(tail[:chunk] + tail[chunk:], 1)
    red = jnp.concatenate([user_red, goods_red])
    spread = lax.all_to_all(
        jnp.broadcast_to(red[None], (devices,) + red.shape), AXES, split_axis=0, concat_axis=0, tiled=True
    )
    user_proj_grad = spread[:, :chunk].reshape(width, width)
    item_proj_grad = spread[:, chunk:].reshape(width, width)
    user_grad = add_rows(rows_dev, user_want, got[:cap])
    item_grad = add_rows(rows_dev, goods_want, got[cap:slots])
    return (user_grad, item_grad, user_proj_grad, item_proj_grad)


def solution(mesh):
    in_specs = (
        P(AXES, None),
        P(AXES, None),
        P(AXES, None),
        P(AXES),
        P(AXES, None),
        P(AXES),
        P(),
        P(AXES, None),
        P(AXES),
        P(),
        P(),
        P(),
    )
    out_specs = (P(AXES, None), P(AXES, None), P(), P())
    return jax.shard_map(local, mesh=mesh, in_specs=in_specs, out_specs=out_specs, check_vma=False)
```

```python
import jax
import jax.numpy as jnp
from jax import lax
from jax.sharding import PartitionSpec as P

EPS = 1e-06
AXES = ("dp", "table")


def tower(x, weight):
    u = jnp.dot(x, weight, preferred_element_type=jnp.float32)
    r = lax.rsqrt(jnp.sum(u * u, -1, keepdims=True) + EPS)
    return (u * r, r)


def slot_rank(owner, devices):
    onehot = (owner[:, None] == jnp.arange(devices, dtype=jnp.int32)[None, :]).astype(jnp.int32)
    before = jnp.cumsum(onehot, 0) - onehot
    return jnp.sum(before * onehot, 1)


def pick_rows(table, wanted):
    rows_dev = table.shape[0]
    flat = wanted.reshape(-1)
    onehot = (flat[:, None] == jnp.arange(rows_dev, dtype=jnp.int32)[None, :]).astype(table.dtype)
    picked = jnp.dot(onehot, table, preferred_element_type=jnp.float32).astype(table.dtype)
    return picked.reshape(wanted.shape + table.shape[1:])


def add_rows(rows_dev, wanted, values):
    flat = wanted.reshape(-1)
    onehot = (jnp.arange(rows_dev, dtype=jnp.int32)[:, None] == flat[None, :]).astype(values.dtype)
    return jnp.dot(onehot, values.reshape(flat.shape[0], -1), preferred_element_type=jnp.float32)


def exchange(x):
    return lax.all_to_all(x, AXES, split_axis=1, concat_axis=1, tiled=True)


def local(
    user_table,
    item_table,
    hist_owner,
    hist_row,
    hist_seg,
    hist_wix,
    bag_weights,
    item_owner,
    item_row,
    user_proj,
    item_proj,
    logit_scale,
):
    rows_dev, width = user_table.shape
    n_dp = lax.axis_size("dp")
    n_tab = lax.axis_size("table")
    devices = n_dp * n_tab
    tokens = hist_row.shape[0]
    samples = item_row.shape[0]
    cap = max(2, 2 * tokens // devices)
    cap_item = max(2, 2 * samples // devices)
    slots = cap + cap_item
    myself = lax.axis_index(AXES)
    entries = bag_weights.shape[0]
    segment = hist_seg[0]
    sample_ids = jnp.arange(samples, dtype=jnp.int32)
    owner = jnp.concatenate([hist_owner[:, 0], item_owner[:, 0]])
    rank = jnp.concatenate(
        [slot_rank(hist_owner[:, 0], devices), cap + slot_rank(item_owner[:, 0], devices)]
    )
    row = jnp.concatenate([hist_row, item_row])
    fields = jnp.stack(
        [
            row & 255,
            row >> 8,
            jnp.concatenate([segment, sample_ids]),
            jnp.concatenate([hist_wix, jnp.zeros((samples,), jnp.int32)]),
            jnp.ones_like(row),
        ]
    )
    by_owner = (owner[None, :] == jnp.arange(devices, dtype=jnp.int32)[:, None]).astype(jnp.bfloat16)
    planes = (fields.astype(jnp.bfloat16)[:, None, :] * by_owner[None, :, :]).reshape(-1, owner.shape[0])
    by_rank = (rank[:, None] == jnp.arange(slots, dtype=jnp.int32)[None, :]).astype(jnp.bfloat16)
    table = jnp.dot(planes, by_rank, preferred_element_type=jnp.float32)
    table = table.astype(jnp.int32).reshape(fields.shape[0], devices, slots)
    table = jnp.transpose(table, (0, 2, 1)).reshape(fields.shape[0], slots * devices)
    slot_row = table[0] + 256 * table[1]
    slot_seg = table[2]
    slot_wix = table[3]
    filled = table[4] > 0
    req = jnp.where(filled, slot_row, rows_dev).reshape(slots, devices)
    is_user = jnp.arange(slots * devices, dtype=jnp.int32) < cap * devices
    want = exchange(req)
    user_want = want[:cap]
    goods_want = want[cap:]
    goods_back = exchange(pick_rows(item_table, goods_want))
    user_back = exchange(pick_rows(user_table, user_want))
    wts = jnp.sum(
        jnp.where(
            slot_wix[:, None] == jnp.arange(entries, dtype=jnp.int32)[None, :],
            bag_weights[None, :].astype(jnp.float32),
            0.0,
        ),
        1,
    ).astype(jnp.bfloat16)
    of_sample = filled[None, :] & (slot_seg[None, :] == sample_ids[:, None])
    item_pick = of_sample[:, cap * devices :].astype(jnp.bfloat16)
    item_emb = jnp.dot(
        item_pick, goods_back.reshape(-1, width), preferred_element_type=jnp.float32
    ).astype(jnp.bfloat16)
    vn, rv = tower(item_emb, item_proj)
    vh = vn.astype(jnp.bfloat16)
    vh_all = lax.all_gather(vh, AXES, axis=0, tiled=True)
    coef = jnp.where(of_sample[:, : cap * devices], wts[None, : cap * devices], jnp.zeros((), jnp.bfloat16))
    numer = jnp.dot(coef, user_back.reshape(-1, width), preferred_element_type=jnp.float32)
    denom = jnp.sum(coef.astype(jnp.float32), 1)
    bag = (numer / denom[:, None]).astype(jnp.bfloat16)
    un, ru = tower(bag, user_proj)
    uh = un.astype(jnp.bfloat16)
    uh_all = lax.all_gather(uh, AXES, axis=0, tiled=True)
    scale = logit_scale[0]
    total = vh_all.shape[0]
    mine = myself * samples + sample_ids
    everyone = jnp.arange(total, dtype=jnp.int32)
    scores = scale * jnp.dot(uh, vh_all.T, preferred_element_type=jnp.float32)
    top = jnp.max(scores, -1)
    expo = jnp.exp(scores - top[:, None])
    norm = jnp.sum(expo, -1)
    prob = expo / norm[:, None]
    hot = (everyone[None, :] == mine[:, None]).astype(jnp.float32)
    pw = (prob - hot).astype(jnp.bfloat16)
    d_un = scale / total * jnp.dot(pw, vh_all, preferred_element_type=jnp.float32)
    d_u = ru * (d_un - un * jnp.sum(un * d_un, -1, keepdims=True))
    highest = lax.Precision.HIGHEST
    user_part = jnp.dot(bag.astype(jnp.float32).T, d_u, precision=highest)
    d_bag = jnp.dot(d_u, user_proj.astype(jnp.float32).T, precision=highest)
    n_user = cap * devices
    pick = jnp.concatenate([d_bag, denom[:, None]], axis=1)
    per_slot = jnp.dot(of_sample[:, :n_user].T.astype(jnp.float32), pick, precision=highest)
    g_slot = (wts[:n_user].astype(jnp.float32) / per_slot[:, width])[:, None] * per_slot[:, :width]
    g_slot = jnp.where(filled[:n_user, None], g_slot, 0.0)
    got_user = exchange(g_slot.astype(jnp.bfloat16).reshape(cap, devices, width))
    user_grad = add_rows(rows_dev, user_want, got_user)
    stats = jnp.concatenate([top, norm]).reshape(1, 1, -1)
    stats = jnp.broadcast_to(stats, (devices, 1, stats.shape[-1]))
    stats = jnp.pad(stats, ((0, 0), (0, 0), (0, -stats.shape[-1] % width)))
    stats = stats.reshape(devices, -1, width)
    user_parts = user_part.reshape(devices, -1, width)
    n_stat = stats.shape[1]
    got_s = lax.all_to_all(
        jnp.concatenate([stats, user_parts], axis=1), AXES, split_axis=0, concat_axis=0, tiled=True
    )
    flat_stats = got_s[:, :n_stat].reshape(devices, -1)
    top_all = flat_stats[:, :samples].reshape(total)
    norm_all = flat_stats[:, samples : 2 * samples].reshape(total)
    user_red = jnp.sum(got_s[:, n_stat:], 0)
    scores_c = scale * jnp.dot(vh, uh_all.T, preferred_element_type=jnp.float32)
    prob_c = jnp.exp(scores_c - top_all[None, :]) / norm_all[None, :]
    hot_c = (everyone[None, :] == mine[:, None]).astype(jnp.float32)
    pw_c = (prob_c - hot_c).astype(jnp.bfloat16)
    d_vn = scale / total * jnp.dot(pw_c, uh_all, preferred_element_type=jnp.float32)
    d_v = rv * (d_vn - vn * jnp.sum(vn * d_vn, -1, keepdims=True))
    goods_part = jnp.dot(item_emb.astype(jnp.float32).T, d_v, precision=highest)
    d_v_slot = jnp.dot(item_pick.T.astype(jnp.float32), d_v, precision=highest)
    goods_parts = jnp.transpose(goods_part.reshape(devices, -1, width), (1, 0, 2))
    chunk = goods_parts.shape[0]
    hi = goods_parts.astype(jnp.bfloat16)
    lo = (goods_parts - hi.astype(jnp.float32)).astype(jnp.bfloat16)
    send = jnp.concatenate(
        [d_v_slot.astype(jnp.bfloat16).reshape(cap_item, devices, width), hi, lo], axis=0
    )
    got = exchange(send)
    tail = got[cap_item:].astype(jnp.float32)
    goods_red = jnp.sum(tail[:chunk] + tail[chunk:], 1)
    red = jnp.concatenate([user_red, goods_red])
    spread = lax.all_to_all(
        jnp.broadcast_to(red[None], (devices,) + red.shape), AXES, split_axis=0, concat_axis=0, tiled=True
    )
    user_proj_grad = spread[:, :chunk].reshape(width, width)
    item_proj_grad = spread[:, chunk:].reshape(width, width)
    item_grad = add_rows(rows_dev, goods_want, got[:cap_item])
    return (user_grad, item_grad, user_proj_grad, item_proj_grad)


def solution(mesh):
    in_specs = (
        P(AXES, None),
        P(AXES, None),
        P(AXES, None),
        P(AXES),
        P(AXES, None),
        P(AXES),
        P(),
        P(AXES, None),
        P(AXES),
        P(),
        P(),
        P(),
    )
    out_specs = (P(AXES, None), P(AXES, None), P(), P())
    return jax.shard_map(local, mesh=mesh, in_specs=in_specs, out_specs=out_specs, check_vma=False)
```

```python
import jax
import jax.numpy as jnp
from jax import lax
from jax.sharding import PartitionSpec as P

EPS = 1e-06
AXES = ("dp", "table")


def tower(x, weight):
    u = jnp.dot(x, weight, preferred_element_type=jnp.float32)
    r = lax.rsqrt(jnp.sum(u * u, -1, keepdims=True) + EPS)
    return (u * r, r)


def slot_rank(owner, devices):
    onehot = (owner[:, None] == jnp.arange(devices, dtype=jnp.int32)[None, :]).astype(jnp.int32)
    before = jnp.cumsum(onehot, 0) - onehot
    return jnp.sum(before * onehot, 1)


def pick_rows(table, wanted):
    rows_dev = table.shape[0]
    flat = wanted.reshape(-1)
    onehot = (flat[:, None] == jnp.arange(rows_dev, dtype=jnp.int32)[None, :]).astype(table.dtype)
    picked = jnp.dot(onehot, table, preferred_element_type=jnp.float32).astype(table.dtype)
    return picked.reshape(wanted.shape + table.shape[1:])


def add_rows(rows_dev, wanted, values):
    flat = wanted.reshape(-1)
    onehot = (jnp.arange(rows_dev, dtype=jnp.int32)[:, None] == flat[None, :]).astype(values.dtype)
    return jnp.dot(onehot, values.reshape(flat.shape[0], -1), preferred_element_type=jnp.float32)


def slot_table(owner, row, extra, nslots, devices):
    rank = slot_rank(owner, devices)
    fields = jnp.stack([row & 255, row >> 8] + extra + [jnp.ones_like(row)])
    by_owner = (owner[None, :] == jnp.arange(devices, dtype=jnp.int32)[:, None]).astype(jnp.bfloat16)
    planes = (fields.astype(jnp.bfloat16)[:, None, :] * by_owner[None, :, :]).reshape(-1, owner.shape[0])
    by_rank = (rank[:, None] == jnp.arange(nslots, dtype=jnp.int32)[None, :]).astype(jnp.bfloat16)
    table = jnp.dot(planes, by_rank, preferred_element_type=jnp.float32)
    table = table.astype(jnp.int32).reshape(fields.shape[0], devices, nslots)
    table = jnp.transpose(table, (0, 2, 1)).reshape(fields.shape[0], nslots * devices)
    slot_row = table[0] + 256 * table[1]
    return jnp.concatenate([slot_row[None], table[2:-1]]), table[-1] > 0


def exchange(x):
    return lax.all_to_all(x, AXES, split_axis=1, concat_axis=1, tiled=True)


def local(
    user_table,
    item_table,
    hist_owner,
    hist_row,
    hist_seg,
    hist_wix,
    bag_weights,
    item_owner,
    item_row,
    user_proj,
    item_proj,
    logit_scale,
):
    rows_dev, width = user_table.shape
    n_dp = lax.axis_size("dp")
    n_tab = lax.axis_size("table")
    devices = n_dp * n_tab
    tokens = hist_row.shape[0]
    samples = item_row.shape[0]
    cap = max(2, 2 * tokens // devices)
    cap_item = max(2, 2 * samples // devices)
    slots = cap + cap_item
    myself = lax.axis_index(AXES)
    entries = bag_weights.shape[0]
    segment = hist_seg[0]
    sample_ids = jnp.arange(samples, dtype=jnp.int32)
    item_fields, item_filled = slot_table(
        item_owner[:, 0], item_row, [sample_ids], cap_item, devices
    )
    goods_want = exchange(jnp.where(item_filled, item_fields[0], rows_dev).reshape(cap_item, devices))
    user_fields, user_filled = slot_table(
        hist_owner[:, 0], hist_row, [segment, hist_wix], cap, devices
    )
    user_want = exchange(jnp.where(user_filled, user_fields[0], rows_dev).reshape(cap, devices))
    slot_seg = jnp.concatenate([user_fields[1], item_fields[1]])
    slot_wix = jnp.concatenate([user_fields[2], jnp.zeros_like(item_fields[1])])
    filled = jnp.concatenate([user_filled, item_filled])
    goods_back = exchange(pick_rows(item_table, goods_want))
    user_back = exchange(pick_rows(user_table, user_want))
    wts = jnp.sum(
        jnp.where(
            slot_wix[:, None] == jnp.arange(entries, dtype=jnp.int32)[None, :],
            bag_weights[None, :].astype(jnp.float32),
            0.0,
        ),
        1,
    ).astype(jnp.bfloat16)
    of_sample = filled[None, :] & (slot_seg[None, :] == sample_ids[:, None])
    item_pick = of_sample[:, cap * devices :].astype(jnp.bfloat16)
    item_emb = jnp.dot(
        item_pick, goods_back.reshape(-1, width), preferred_element_type=jnp.float32
    ).astype(jnp.bfloat16)
    vn, rv = tower(item_emb, item_proj)
    vh = vn.astype(jnp.bfloat16)
    vh_all = lax.all_gather(vh, AXES, axis=0, tiled=True)
    coef = jnp.where(of_sample[:, : cap * devices], wts[None, : cap * devices], jnp.zeros((), jnp.bfloat16))
    numer = jnp.dot(coef, user_back.reshape(-1, width), preferred_element_type=jnp.float32)
    denom = jnp.sum(coef.astype(jnp.float32), 1)
    bag = (numer / denom[:, None]).astype(jnp.bfloat16)
    un, ru = tower(bag, user_proj)
    uh = un.astype(jnp.bfloat16)
    uh_all = lax.all_gather(uh, AXES, axis=0, tiled=True)
    scale = logit_scale[0]
    total = vh_all.shape[0]
    mine = myself * samples + sample_ids
    everyone = jnp.arange(total, dtype=jnp.int32)
    scores = scale * jnp.dot(uh, vh_all.T, preferred_element_type=jnp.float32)
    top = jnp.max(scores, -1)
    expo = jnp.exp(scores - top[:, None])
    norm = jnp.sum(expo, -1)
    prob = expo / norm[:, None]
    hot = (everyone[None, :] == mine[:, None]).astype(jnp.float32)
    pw = (prob - hot).astype(jnp.bfloat16)
    d_un = scale / total * jnp.dot(pw, vh_all, preferred_element_type=jnp.float32)
    d_u = ru * (d_un - un * jnp.sum(un * d_un, -1, keepdims=True))
    highest = lax.Precision.HIGHEST
    user_part = jnp.dot(bag.astype(jnp.float32).T, d_u, precision=highest)
    d_bag = jnp.dot(d_u, user_proj.astype(jnp.float32).T, precision=highest)
    n_user = cap * devices
    pick = jnp.concatenate([d_bag, denom[:, None]], axis=1)
    per_slot = jnp.dot(of_sample[:, :n_user].T.astype(jnp.float32), pick, precision=highest)
    g_slot = (wts[:n_user].astype(jnp.float32) / per_slot[:, width])[:, None] * per_slot[:, :width]
    g_slot = jnp.where(filled[:n_user, None], g_slot, 0.0)
    got_user = exchange(g_slot.astype(jnp.bfloat16).reshape(cap, devices, width))
    user_grad = add_rows(rows_dev, user_want, got_user)
    stats = jnp.concatenate([top, norm]).reshape(1, 1, -1)
    stats = jnp.broadcast_to(stats, (devices, 1, stats.shape[-1]))
    stats = jnp.pad(stats, ((0, 0), (0, 0), (0, -stats.shape[-1] % width)))
    stats = stats.reshape(devices, -1, width)
    user_parts = user_part.reshape(devices, -1, width)
    n_stat = stats.shape[1]
    got_s = lax.all_to_all(
        jnp.concatenate([stats, user_parts], axis=1), AXES, split_axis=0, concat_axis=0, tiled=True
    )
    flat_stats = got_s[:, :n_stat].reshape(devices, -1)
    top_all = flat_stats[:, :samples].reshape(total)
    norm_all = flat_stats[:, samples : 2 * samples].reshape(total)
    user_red = jnp.sum(got_s[:, n_stat:], 0)
    scores_c = scale * jnp.dot(vh, uh_all.T, preferred_element_type=jnp.float32)
    prob_c = jnp.exp(scores_c - top_all[None, :]) / norm_all[None, :]
    hot_c = (everyone[None, :] == mine[:, None]).astype(jnp.float32)
    pw_c = (prob_c - hot_c).astype(jnp.bfloat16)
    d_vn = scale / total * jnp.dot(pw_c, uh_all, preferred_element_type=jnp.float32)
    d_v = rv * (d_vn - vn * jnp.sum(vn * d_vn, -1, keepdims=True))
    goods_part = jnp.dot(item_emb.astype(jnp.float32).T, d_v, precision=highest)
    d_v_slot = jnp.dot(item_pick.T.astype(jnp.float32), d_v, precision=highest)
    goods_parts = jnp.transpose(goods_part.reshape(devices, -1, width), (1, 0, 2))
    chunk = goods_parts.shape[0]
    hi = goods_parts.astype(jnp.bfloat16)
    lo = (goods_parts - hi.astype(jnp.float32)).astype(jnp.bfloat16)
    send = jnp.concatenate(
        [d_v_slot.astype(jnp.bfloat16).reshape(cap_item, devices, width), hi, lo], axis=0
    )
    got = exchange(send)
    tail = got[cap_item:].astype(jnp.float32)
    goods_red = jnp.sum(tail[:chunk] + tail[chunk:], 1)
    red = jnp.concatenate([user_red, goods_red])
    spread = lax.all_to_all(
        jnp.broadcast_to(red[None], (devices,) + red.shape), AXES, split_axis=0, concat_axis=0, tiled=True
    )
    user_proj_grad = spread[:, :chunk].reshape(width, width)
    item_proj_grad = spread[:, chunk:].reshape(width, width)
    item_grad = add_rows(rows_dev, goods_want, got[:cap_item])
    return (user_grad, item_grad, user_proj_grad, item_proj_grad)


def solution(mesh):
    in_specs = (
        P(AXES, None),
        P(AXES, None),
        P(AXES, None),
        P(AXES),
        P(AXES, None),
        P(AXES),
        P(),
        P(AXES, None),
        P(AXES),
        P(),
        P(),
        P(),
    )
    out_specs = (P(AXES, None), P(AXES, None), P(), P())
    return jax.shard_map(local, mesh=mesh, in_specs=in_specs, out_specs=out_specs, check_vma=False)
```

```python
import jax
import jax.numpy as jnp
from jax import lax
from jax.sharding import PartitionSpec as P

EPS = 1e-06
AXES = ("dp", "table")


def tower(x, weight):
    u = jnp.dot(x, weight, preferred_element_type=jnp.float32)
    r = lax.rsqrt(jnp.sum(u * u, -1, keepdims=True) + EPS)
    return (u * r, r)


def slot_rank(owner, devices):
    onehot = (owner[:, None] == jnp.arange(devices, dtype=jnp.int32)[None, :]).astype(jnp.int32)
    before = jnp.cumsum(onehot, 0) - onehot
    return jnp.sum(before * onehot, 1)


def pick_rows(table, wanted):
    rows_dev = table.shape[0]
    flat = wanted.reshape(-1)
    onehot = (flat[:, None] == jnp.arange(rows_dev, dtype=jnp.int32)[None, :]).astype(table.dtype)
    picked = jnp.dot(onehot, table, preferred_element_type=jnp.float32).astype(table.dtype)
    return picked.reshape(wanted.shape + table.shape[1:])


def add_rows(rows_dev, wanted, values):
    flat = wanted.reshape(-1)
    onehot = (jnp.arange(rows_dev, dtype=jnp.int32)[:, None] == flat[None, :]).astype(values.dtype)
    return jnp.dot(onehot, values.reshape(flat.shape[0], -1), preferred_element_type=jnp.float32)


def exchange(x):
    return lax.all_to_all(x, AXES, split_axis=1, concat_axis=1, tiled=True)


def local(
    user_table,
    item_table,
    hist_owner,
    hist_row,
    hist_seg,
    hist_wix,
    bag_weights,
    item_owner,
    item_row,
    user_proj,
    item_proj,
    logit_scale,
):
    rows_dev, width = user_table.shape
    n_dp = lax.axis_size("dp")
    n_tab = lax.axis_size("table")
    devices = n_dp * n_tab
    tokens = hist_row.shape[0]
    samples = item_row.shape[0]
    cap = max(2, 2 * tokens // devices)
    cap_item = max(2, 2 * samples // devices)
    slots = cap + cap_item
    myself = lax.axis_index(AXES)
    entries = bag_weights.shape[0]
    segment = hist_seg[0]
    sample_ids = jnp.arange(samples, dtype=jnp.int32)
    owner = jnp.concatenate([hist_owner[:, 0], item_owner[:, 0]])
    rank = jnp.concatenate(
        [slot_rank(hist_owner[:, 0], devices), cap + slot_rank(item_owner[:, 0], devices)]
    )
    row = jnp.concatenate([hist_row, item_row])
    fields = jnp.stack(
        [
            row & 255,
            row >> 8,
            jnp.concatenate([segment, sample_ids]),
            jnp.concatenate([hist_wix, jnp.zeros((samples,), jnp.int32)]),
            jnp.ones_like(row),
        ]
    )
    by_owner = (owner[None, :] == jnp.arange(devices, dtype=jnp.int32)[:, None]).astype(jnp.bfloat16)
    planes = (fields.astype(jnp.bfloat16)[:, None, :] * by_owner[None, :, :]).reshape(-1, owner.shape[0])
    by_rank = (rank[:, None] == jnp.arange(slots, dtype=jnp.int32)[None, :]).astype(jnp.bfloat16)
    table = jnp.dot(planes, by_rank, preferred_element_type=jnp.float32)
    table = table.astype(jnp.int32).reshape(fields.shape[0], devices, slots)
    table = jnp.transpose(table, (0, 2, 1)).reshape(fields.shape[0], slots * devices)
    slot_row = table[0] + 256 * table[1]
    slot_seg = table[2]
    slot_wix = table[3]
    filled = table[4] > 0
    req = jnp.where(filled, slot_row, rows_dev).reshape(slots, devices)
    is_user = jnp.arange(slots * devices, dtype=jnp.int32) < cap * devices
    want = exchange(req)
    user_want = want[:cap]
    goods_want = want[cap:]
    goods_back = exchange(pick_rows(item_table, goods_want))
    user_back = exchange(pick_rows(user_table, user_want))
    wts = jnp.sum(
        jnp.where(
            slot_wix[:, None] == jnp.arange(entries, dtype=jnp.int32)[None, :],
            bag_weights[None, :].astype(jnp.float32),
            0.0,
        ),
        1,
    ).astype(jnp.bfloat16)
    of_sample = filled[None, :] & (slot_seg[None, :] == sample_ids[:, None])
    item_pick = of_sample[:, cap * devices :].astype(jnp.bfloat16)
    item_emb = jnp.dot(
        item_pick, goods_back.reshape(-1, width), preferred_element_type=jnp.float32
    ).astype(jnp.bfloat16)
    vn, rv = tower(item_emb, item_proj)
    vh = vn.astype(jnp.bfloat16)
    vh_all = lax.all_gather(vh, AXES, axis=0, tiled=True)
    coef = jnp.where(of_sample[:, : cap * devices], wts[None, : cap * devices], jnp.zeros((), jnp.bfloat16))
    numer = jnp.dot(coef, user_back.reshape(-1, width), preferred_element_type=jnp.float32)
    denom = jnp.sum(coef.astype(jnp.float32), 1)
    bag = (numer / denom[:, None]).astype(jnp.bfloat16)
    un, ru = tower(bag, user_proj)
    uh = un.astype(jnp.bfloat16)
    uh_all = lax.all_gather(uh, AXES, axis=0, tiled=True)
    scale = logit_scale[0]
    total = vh_all.shape[0]
    mine = myself * samples + sample_ids
    everyone = jnp.arange(total, dtype=jnp.int32)
    scores = scale * jnp.dot(uh, vh_all.T, preferred_element_type=jnp.float32)
    top = jnp.max(scores, -1)
    expo = jnp.exp(scores - top[:, None])
    norm = jnp.sum(expo, -1)
    prob = expo / norm[:, None]
    hot = (everyone[None, :] == mine[:, None]).astype(jnp.float32)
    pw = (prob - hot).astype(jnp.bfloat16)
    d_un = scale / total * jnp.dot(pw, vh_all, preferred_element_type=jnp.float32)
    d_u = ru * (d_un - un * jnp.sum(un * d_un, -1, keepdims=True))
    highest = lax.Precision.HIGHEST
    user_part = jnp.dot(bag.astype(jnp.float32).T, d_u, precision=highest)
    d_bag = jnp.dot(d_u, user_proj.astype(jnp.float32).T, precision=highest)
    n_user = cap * devices
    pick = jnp.concatenate([d_bag, denom[:, None]], axis=1)
    per_slot = jnp.dot(of_sample[:, :n_user].T.astype(jnp.float32), pick, precision=highest)
    g_slot = (wts[:n_user].astype(jnp.float32) / per_slot[:, width])[:, None] * per_slot[:, :width]
    g_slot = jnp.where(filled[:n_user, None], g_slot, 0.0)
    got_user = exchange(g_slot.astype(jnp.bfloat16).reshape(cap, devices, width))
    user_grad = add_rows(rows_dev, user_want, got_user)
    stats = jnp.concatenate([top, norm]).reshape(1, 1, -1)
    stats = jnp.broadcast_to(stats, (devices, 1, stats.shape[-1]))
    stats = jnp.pad(stats, ((0, 0), (0, 0), (0, -stats.shape[-1] % width)))
    stats = stats.reshape(devices, -1, width)
    user_parts = jnp.transpose(user_part.reshape(-1, devices, width), (1, 0, 2))
    n_stat = stats.shape[1]
    got_s = lax.all_to_all(
        jnp.concatenate([stats, user_parts], axis=1), AXES, split_axis=0, concat_axis=0, tiled=True
    )
    flat_stats = got_s[:, :n_stat].reshape(devices, -1)
    top_all = flat_stats[:, :samples].reshape(total)
    norm_all = flat_stats[:, samples : 2 * samples].reshape(total)
    user_red = jnp.sum(got_s[:, n_stat:], 0)
    scores_c = scale * jnp.dot(vh, uh_all.T, preferred_element_type=jnp.float32)
    prob_c = jnp.exp(scores_c - top_all[None, :]) * (1.0 / norm_all)[None, :]
    hot_c = (everyone[None, :] == mine[:, None]).astype(jnp.float32)
    pw_c = (prob_c - hot_c).astype(jnp.bfloat16)
    d_vn = scale / total * jnp.dot(pw_c, uh_all, preferred_element_type=jnp.float32)
    d_v = rv * (d_vn - vn * jnp.sum(vn * d_vn, -1, keepdims=True))
    goods_part = jnp.dot(item_emb.astype(jnp.float32).T, d_v, precision=highest)
    d_v_slot = jnp.dot(item_pick.T.astype(jnp.float32), d_v, precision=highest)
    goods_parts = goods_part.reshape(-1, devices, width)
    chunk = goods_parts.shape[0]
    hi = goods_parts.astype(jnp.bfloat16)
    lo = (goods_parts - hi.astype(jnp.float32)).astype(jnp.bfloat16)
    send = jnp.concatenate(
        [d_v_slot.astype(jnp.bfloat16).reshape(cap_item, devices, width), hi, lo], axis=0
    )
    got = exchange(send)
    tail = got[cap_item:].astype(jnp.float32)
    goods_red = jnp.sum(tail[:chunk] + tail[chunk:], 1)
    red = jnp.concatenate([user_red, goods_red])
    spread = exchange(jnp.broadcast_to(red[:, None], (red.shape[0], devices, width)))
    user_proj_grad = spread[:chunk].reshape(width, width)
    item_proj_grad = spread[chunk:].reshape(width, width)
    item_grad = add_rows(rows_dev, goods_want, got[:cap_item])
    return (user_grad, item_grad, user_proj_grad, item_proj_grad)


def solution(mesh):
    in_specs = (
        P(AXES, None),
        P(AXES, None),
        P(AXES, None),
        P(AXES),
        P(AXES, None),
        P(AXES),
        P(),
        P(AXES, None),
        P(AXES),
        P(),
        P(),
        P(),
    )
    out_specs = (P(AXES, None), P(AXES, None), P(), P())
    return jax.shard_map(local, mesh=mesh, in_specs=in_specs, out_specs=out_specs, check_vma=False)
```

```python
import jax
import jax.numpy as jnp
from jax import lax
from jax.sharding import PartitionSpec as P
from jax.experimental import pallas as pl
from jax.experimental.pallas import tpu as pltpu

EPS = 1e-06
AXES = ("dp", "table")


def tower(x, weight):
    u = jnp.dot(x, weight, preferred_element_type=jnp.float32)
    r = lax.rsqrt(jnp.sum(u * u, -1, keepdims=True) + EPS)
    return (u * r, r)


def slot_rank(owner, devices):
    onehot = (owner[:, None] == jnp.arange(devices, dtype=jnp.int32)[None, :]).astype(jnp.int32)
    before = jnp.cumsum(onehot, 0) - onehot
    return jnp.sum(before * onehot, 1)


def pick_rows(table, wanted):
    rows_dev = table.shape[0]
    flat = wanted.reshape(-1)
    onehot = (flat[:, None] == jnp.arange(rows_dev, dtype=jnp.int32)[None, :]).astype(table.dtype)
    picked = jnp.dot(onehot, table, preferred_element_type=jnp.float32).astype(table.dtype)
    return picked.reshape(wanted.shape + table.shape[1:])


def add_rows(rows_dev, wanted, values):
    flat = wanted.reshape(-1)
    onehot = (jnp.arange(rows_dev, dtype=jnp.int32)[:, None] == flat[None, :]).astype(values.dtype)
    return jnp.dot(onehot, values.reshape(flat.shape[0], -1), preferred_element_type=jnp.float32)


def exchange(x):
    return lax.all_to_all(x, AXES, split_axis=1, concat_axis=1, tiled=True)


def _column_kernel(base_ref, scale_ref, vh_ref, uh_ref, top_ref, norm_ref, out_ref, acc_ref):
    b = pl.program_id(0)
    rows, block = vh_ref.shape[0], uh_ref.shape[0]

    @pl.when(b == 0)
    def _():
        acc_ref[...] = jnp.zeros_like(acc_ref)

    uh = uh_ref[...]
    s = scale_ref[0] * lax.dot_general(
        vh_ref[...], uh, (((1,), (1,)), ((), ())), preferred_element_type=jnp.float32
    )
    p = jnp.exp(s - top_ref[...]) / norm_ref[...]
    col = b * block + lax.broadcasted_iota(jnp.int32, (rows, block), 1)
    mine = base_ref[0] + lax.broadcasted_iota(jnp.int32, (rows, block), 0)
    pw = (p - (col == mine).astype(jnp.float32)).astype(jnp.bfloat16)
    acc_ref[...] += jnp.dot(pw, uh, preferred_element_type=jnp.float32)

    @pl.when(b == pl.num_programs(0) - 1)
    def _():
        out_ref[...] = acc_ref[...]


def column_side(base, scale, vh, uh_all, top_all, norm_all, block=2048):
    rows, width = vh.shape
    total = uh_all.shape[0]
    grid_spec = pltpu.PrefetchScalarGridSpec(
        num_scalar_prefetch=1,
        grid=(total // block,),
        in_specs=[
            pl.BlockSpec(memory_space=pltpu.SMEM),
            pl.BlockSpec((rows, width), lambda b, base: (0, 0)),
            pl.BlockSpec((block, width), lambda b, base: (b, 0)),
            pl.BlockSpec((1, block), lambda b, base: (0, b)),
            pl.BlockSpec((1, block), lambda b, base: (0, b)),
        ],
        out_specs=pl.BlockSpec((rows, width), lambda b, base: (0, 0)),
        scratch_shapes=[pltpu.VMEM((rows, width), jnp.float32)],
    )
    return pl.pallas_call(
        _column_kernel,
        out_shape=jax.ShapeDtypeStruct((rows, width), jnp.float32),
        grid_spec=grid_spec,
        compiler_params=pltpu.CompilerParams(dimension_semantics=("arbitrary",)),
    )(base.reshape(1), scale.reshape(1), vh, uh_all, top_all[None], norm_all[None])


def local(
    user_table,
    item_table,
    hist_owner,
    hist_row,
    hist_seg,
    hist_wix,
    bag_weights,
    item_owner,
    item_row,
    user_proj,
    item_proj,
    logit_scale,
):
    rows_dev, width = user_table.shape
    n_dp = lax.axis_size("dp")
    n_tab = lax.axis_size("table")
    devices = n_dp * n_tab
    tokens = hist_row.shape[0]
    samples = item_row.shape[0]
    cap = max(2, 2 * tokens // devices)
    cap_item = max(2, 2 * samples // devices)
    slots = cap + cap_item
    myself = lax.axis_index(AXES)
    entries = bag_weights.shape[0]
    segment = hist_seg[0]
    sample_ids = jnp.arange(samples, dtype=jnp.int32)
    owner = jnp.concatenate([hist_owner[:, 0], item_owner[:, 0]])
    rank = jnp.concatenate(
        [slot_rank(hist_owner[:, 0], devices), cap + slot_rank(item_owner[:, 0], devices)]
    )
    row = jnp.concatenate([hist_row, item_row])
    fields = jnp.stack(
        [
            row & 255,
            row >> 8,
            jnp.concatenate([segment, sample_ids]),
            jnp.concatenate([hist_wix, jnp.zeros((samples,), jnp.int32)]),
            jnp.ones_like(row),
        ]
    )
    by_owner = (owner[None, :] == jnp.arange(devices, dtype=jnp.int32)[:, None]).astype(jnp.bfloat16)
    planes = (fields.astype(jnp.bfloat16)[:, None, :] * by_owner[None, :, :]).reshape(-1, owner.shape[0])
    by_rank = (rank[:, None] == jnp.arange(slots, dtype=jnp.int32)[None, :]).astype(jnp.bfloat16)
    table = jnp.dot(planes, by_rank, preferred_element_type=jnp.float32)
    table = table.astype(jnp.int32).reshape(fields.shape[0], devices, slots)
    table = jnp.transpose(table, (0, 2, 1)).reshape(fields.shape[0], slots * devices)
    slot_row = table[0] + 256 * table[1]
    slot_seg = table[2]
    slot_wix = table[3]
    filled = table[4] > 0
    req = jnp.where(filled, slot_row, rows_dev).reshape(slots, devices)
    is_user = jnp.arange(slots * devices, dtype=jnp.int32) < cap * devices
    want = exchange(req)
    user_want = want[:cap]
    goods_want = want[cap:]
    goods_back = exchange(pick_rows(item_table, goods_want))
    user_back = exchange(pick_rows(user_table, user_want))
    wts = jnp.sum(
        jnp.where(
            slot_wix[:, None] == jnp.arange(entries, dtype=jnp.int32)[None, :],
            bag_weights[None, :].astype(jnp.float32),
            0.0,
        ),
        1,
    ).astype(jnp.bfloat16)
    of_sample = filled[None, :] & (slot_seg[None, :] == sample_ids[:, None])
    item_pick = of_sample[:, cap * devices :].astype(jnp.bfloat16)
    item_emb = jnp.dot(
        item_pick, goods_back.reshape(-1, width), preferred_element_type=jnp.float32
    ).astype(jnp.bfloat16)
    vn, rv = tower(item_emb, item_proj)
    vh = vn.astype(jnp.bfloat16)
    vh_all = lax.all_gather(vh, AXES, axis=0, tiled=True)
    coef = jnp.where(of_sample[:, : cap * devices], wts[None, : cap * devices], jnp.zeros((), jnp.bfloat16))
    numer = jnp.dot(coef, user_back.reshape(-1, width), preferred_element_type=jnp.float32)
    denom = jnp.sum(coef.astype(jnp.float32), 1)
    bag = (numer / denom[:, None]).astype(jnp.bfloat16)
    un, ru = tower(bag, user_proj)
    uh = un.astype(jnp.bfloat16)
    uh_all = lax.all_gather(uh, AXES, axis=0, tiled=True)
    scale = logit_scale[0]
    total = vh_all.shape[0]
    mine = myself * samples + sample_ids
    everyone = jnp.arange(total, dtype=jnp.int32)
    scores = scale * jnp.dot(uh, vh_all.T, preferred_element_type=jnp.float32)
    top = jnp.max(scores, -1)
    expo = jnp.exp(scores - top[:, None])
    norm = jnp.sum(expo, -1)
    prob = expo / norm[:, None]
    hot = (everyone[None, :] == mine[:, None]).astype(jnp.float32)
    pw = (prob - hot).astype(jnp.bfloat16)
    d_un = scale / total * jnp.dot(pw, vh_all, preferred_element_type=jnp.float32)
    d_u = ru * (d_un - un * jnp.sum(un * d_un, -1, keepdims=True))
    highest = lax.Precision.HIGHEST
    user_part = jnp.dot(bag.astype(jnp.float32).T, d_u, precision=highest)
    d_bag = jnp.dot(d_u, user_proj.astype(jnp.float32).T, precision=highest)
    n_user = cap * devices
    pick = jnp.concatenate([d_bag, denom[:, None]], axis=1)
    per_slot = jnp.dot(of_sample[:, :n_user].T.astype(jnp.float32), pick, precision=highest)
    g_slot = (wts[:n_user].astype(jnp.float32) / per_slot[:, width])[:, None] * per_slot[:, :width]
    g_slot = jnp.where(filled[:n_user, None], g_slot, 0.0)
    got_user = exchange(g_slot.astype(jnp.bfloat16).reshape(cap, devices, width))
    user_grad = add_rows(rows_dev, user_want, got_user)
    stats = jnp.concatenate([top, norm]).reshape(1, 1, -1)
    stats = jnp.broadcast_to(stats, (devices, 1, stats.shape[-1]))
    stats = jnp.pad(stats, ((0, 0), (0, 0), (0, -stats.shape[-1] % width)))
    stats = stats.reshape(devices, -1, width)
    user_parts = user_part.reshape(devices, -1, width)
    n_stat = stats.shape[1]
    got_s = lax.all_to_all(
        jnp.concatenate([stats, user_parts], axis=1), AXES, split_axis=0, concat_axis=0, tiled=True
    )
    flat_stats = got_s[:, :n_stat].reshape(devices, -1)
    top_all = flat_stats[:, :samples].reshape(total)
    norm_all = flat_stats[:, samples : 2 * samples].reshape(total)
    user_red = jnp.sum(got_s[:, n_stat:], 0)
    d_vn = scale / total * column_side(myself * samples, scale, vh, uh_all, top_all, norm_all)
    d_v = rv * (d_vn - vn * jnp.sum(vn * d_vn, -1, keepdims=True))
    goods_part = jnp.dot(item_emb.astype(jnp.float32).T, d_v, precision=highest)
    d_v_slot = jnp.dot(item_pick.T.astype(jnp.float32), d_v, precision=highest)
    goods_parts = jnp.transpose(goods_part.reshape(devices, -1, width), (1, 0, 2))
    chunk = goods_parts.shape[0]
    hi = goods_parts.astype(jnp.bfloat16)
    lo = (goods_parts - hi.astype(jnp.float32)).astype(jnp.bfloat16)
    send = jnp.concatenate(
        [d_v_slot.astype(jnp.bfloat16).reshape(cap_item, devices, width), hi, lo], axis=0
    )
    got = exchange(send)
    tail = got[cap_item:].astype(jnp.float32)
    goods_red = jnp.sum(tail[:chunk] + tail[chunk:], 1)
    red = jnp.concatenate([user_red, goods_red])
    spread = lax.all_to_all(
        jnp.broadcast_to(red[None], (devices,) + red.shape), AXES, split_axis=0, concat_axis=0, tiled=True
    )
    user_proj_grad = spread[:, :chunk].reshape(width, width)
    item_proj_grad = spread[:, chunk:].reshape(width, width)
    item_grad = add_rows(rows_dev, goods_want, got[:cap_item])
    return (user_grad, item_grad, user_proj_grad, item_proj_grad)


def solution(mesh):
    in_specs = (
        P(AXES, None),
        P(AXES, None),
        P(AXES, None),
        P(AXES),
        P(AXES, None),
        P(AXES),
        P(),
        P(AXES, None),
        P(AXES),
        P(),
        P(),
        P(),
    )
    out_specs = (P(AXES, None), P(AXES, None), P(), P())
    return jax.shard_map(local, mesh=mesh, in_specs=in_specs, out_specs=out_specs, check_vma=False)
```

```python
import jax
import jax.numpy as jnp
from jax import lax
from jax.sharding import PartitionSpec as P
from jax.experimental import pallas as pl
from jax.experimental.pallas import tpu as pltpu

EPS = 1e-06
AXES = ("dp", "table")


def tower(x, weight):
    u = jnp.dot(x, weight, preferred_element_type=jnp.float32)
    r = lax.rsqrt(jnp.sum(u * u, -1, keepdims=True) + EPS)
    return (u * r, r)


def slot_rank(owner, devices):
    onehot = (owner[:, None] == jnp.arange(devices, dtype=jnp.int32)[None, :]).astype(jnp.int32)
    before = jnp.cumsum(onehot, 0) - onehot
    return jnp.sum(before * onehot, 1)


def pick_rows(table, wanted):
    rows_dev = table.shape[0]
    flat = wanted.reshape(-1)
    onehot = (flat[:, None] == jnp.arange(rows_dev, dtype=jnp.int32)[None, :]).astype(table.dtype)
    picked = jnp.dot(onehot, table, preferred_element_type=jnp.float32).astype(table.dtype)
    return picked.reshape(wanted.shape + table.shape[1:])


def add_rows(rows_dev, wanted, values):
    flat = wanted.reshape(-1)
    onehot = (jnp.arange(rows_dev, dtype=jnp.int32)[:, None] == flat[None, :]).astype(values.dtype)
    return jnp.dot(onehot, values.reshape(flat.shape[0], -1), preferred_element_type=jnp.float32)


def exchange(x):
    return lax.all_to_all(x, AXES, split_axis=1, concat_axis=1, tiled=True)


def _column_kernel(base_ref, scale_ref, vh_ref, uh_ref, top_ref, norm_ref, out_ref, acc_ref):
    b = pl.program_id(0)
    rows, block = vh_ref.shape[0], uh_ref.shape[0]

    @pl.when(b == 0)
    def _():
        acc_ref[...] = jnp.zeros_like(acc_ref)

    uh = uh_ref[...]
    s = scale_ref[0] * lax.dot_general(
        vh_ref[...], uh, (((1,), (1,)), ((), ())), preferred_element_type=jnp.float32
    )
    p = jnp.exp(s - top_ref[...]) * (1.0 / norm_ref[...])
    col = b * block + lax.broadcasted_iota(jnp.int32, (rows, block), 1)
    mine = base_ref[0] + lax.broadcasted_iota(jnp.int32, (rows, block), 0)
    pw = (p - (col == mine).astype(jnp.float32)).astype(jnp.bfloat16)
    acc_ref[...] += jnp.dot(pw, uh, preferred_element_type=jnp.float32)

    @pl.when(b == pl.num_programs(0) - 1)
    def _():
        out_ref[...] = acc_ref[...]


def column_side(base, scale, vh, uh_all, top_all, norm_all, block=2048):
    rows, width = vh.shape
    total = uh_all.shape[0]
    grid_spec = pltpu.PrefetchScalarGridSpec(
        num_scalar_prefetch=1,
        grid=(total // block,),
        in_specs=[
            pl.BlockSpec(memory_space=pltpu.SMEM),
            pl.BlockSpec((rows, width), lambda b, base: (0, 0)),
            pl.BlockSpec((block, width), lambda b, base: (b, 0)),
            pl.BlockSpec((1, block), lambda b, base: (0, b)),
            pl.BlockSpec((1, block), lambda b, base: (0, b)),
        ],
        out_specs=pl.BlockSpec((rows, width), lambda b, base: (0, 0)),
        scratch_shapes=[pltpu.VMEM((rows, width), jnp.float32)],
    )
    return pl.pallas_call(
        _column_kernel,
        out_shape=jax.ShapeDtypeStruct((rows, width), jnp.float32),
        grid_spec=grid_spec,
        compiler_params=pltpu.CompilerParams(dimension_semantics=("arbitrary",)),
    )(base.reshape(1), scale.reshape(1), vh, uh_all, top_all[None], norm_all[None])


def local(
    user_table,
    item_table,
    hist_owner,
    hist_row,
    hist_seg,
    hist_wix,
    bag_weights,
    item_owner,
    item_row,
    user_proj,
    item_proj,
    logit_scale,
):
    rows_dev, width = user_table.shape
    n_dp = lax.axis_size("dp")
    n_tab = lax.axis_size("table")
    devices = n_dp * n_tab
    tokens = hist_row.shape[0]
    samples = item_row.shape[0]
    cap = max(2, 2 * tokens // devices)
    cap_item = max(2, 2 * samples // devices)
    slots = cap + cap_item
    myself = lax.axis_index(AXES)
    entries = bag_weights.shape[0]
    segment = hist_seg[0]
    sample_ids = jnp.arange(samples, dtype=jnp.int32)
    owner = jnp.concatenate([hist_owner[:, 0], item_owner[:, 0]])
    rank = jnp.concatenate(
        [slot_rank(hist_owner[:, 0], devices), cap + slot_rank(item_owner[:, 0], devices)]
    )
    row = jnp.concatenate([hist_row, item_row])
    fields = jnp.stack(
        [
            row & 255,
            row >> 8,
            jnp.concatenate([segment, sample_ids]),
            jnp.concatenate([hist_wix, jnp.zeros((samples,), jnp.int32)]),
            jnp.ones_like(row),
        ]
    )
    by_owner = (owner[None, :] == jnp.arange(devices, dtype=jnp.int32)[:, None]).astype(jnp.bfloat16)
    planes = (fields.astype(jnp.bfloat16)[:, None, :] * by_owner[None, :, :]).reshape(-1, owner.shape[0])
    by_rank = (rank[:, None] == jnp.arange(slots, dtype=jnp.int32)[None, :]).astype(jnp.bfloat16)
    table = jnp.dot(planes, by_rank, preferred_element_type=jnp.float32)
    table = table.astype(jnp.int32).reshape(fields.shape[0], devices, slots)
    table = jnp.transpose(table, (0, 2, 1)).reshape(fields.shape[0], slots * devices)
    slot_row = table[0] + 256 * table[1]
    slot_seg = table[2]
    slot_wix = table[3]
    filled = table[4] > 0
    req = jnp.where(filled, slot_row, rows_dev).reshape(slots, devices)
    is_user = jnp.arange(slots * devices, dtype=jnp.int32) < cap * devices
    want = exchange(req)
    user_want = want[:cap]
    goods_want = want[cap:]
    goods_back = exchange(pick_rows(item_table, goods_want))
    user_back = exchange(pick_rows(user_table, user_want))
    wts = jnp.sum(
        jnp.where(
            slot_wix[:, None] == jnp.arange(entries, dtype=jnp.int32)[None, :],
            bag_weights[None, :].astype(jnp.float32),
            0.0,
        ),
        1,
    ).astype(jnp.bfloat16)
    of_sample = filled[None, :] & (slot_seg[None, :] == sample_ids[:, None])
    item_pick = of_sample[:, cap * devices :].astype(jnp.bfloat16)
    item_emb = jnp.dot(
        item_pick, goods_back.reshape(-1, width), preferred_element_type=jnp.float32
    ).astype(jnp.bfloat16)
    vn, rv = tower(item_emb, item_proj)
    vh = vn.astype(jnp.bfloat16)
    vh_all = lax.all_gather(vh, AXES, axis=0, tiled=True)
    coef = jnp.where(of_sample[:, : cap * devices], wts[None, : cap * devices], jnp.zeros((), jnp.bfloat16))
    numer = jnp.dot(coef, user_back.reshape(-1, width), preferred_element_type=jnp.float32)
    denom = jnp.sum(coef.astype(jnp.float32), 1)
    bag = (numer / denom[:, None]).astype(jnp.bfloat16)
    un, ru = tower(bag, user_proj)
    uh = un.astype(jnp.bfloat16)
    uh_all = lax.all_gather(uh, AXES, axis=0, tiled=True)
    scale = logit_scale[0]
    total = vh_all.shape[0]
    mine = myself * samples + sample_ids
    everyone = jnp.arange(total, dtype=jnp.int32)
    scores = scale * jnp.dot(uh, vh_all.T, preferred_element_type=jnp.float32)
    top = jnp.max(scores, -1)
    expo = jnp.exp(scores - top[:, None])
    norm = jnp.sum(expo, -1)
    prob = expo / norm[:, None]
    hot = (everyone[None, :] == mine[:, None]).astype(jnp.float32)
    pw = (prob - hot).astype(jnp.bfloat16)
    d_un = scale / total * jnp.dot(pw, vh_all, preferred_element_type=jnp.float32)
    d_u = ru * (d_un - un * jnp.sum(un * d_un, -1, keepdims=True))
    highest = lax.Precision.HIGHEST
    user_part = jnp.dot(bag.astype(jnp.float32).T, d_u, precision=highest)
    d_bag = jnp.dot(d_u, user_proj.astype(jnp.float32).T, precision=highest)
    n_user = cap * devices
    pick = jnp.concatenate([d_bag, denom[:, None]], axis=1)
    per_slot = jnp.dot(of_sample[:, :n_user].T.astype(jnp.float32), pick, precision=highest)
    g_slot = (wts[:n_user].astype(jnp.float32) / per_slot[:, width])[:, None] * per_slot[:, :width]
    g_slot = jnp.where(filled[:n_user, None], g_slot, 0.0)
    got_user = exchange(g_slot.astype(jnp.bfloat16).reshape(cap, devices, width))
    user_grad = add_rows(rows_dev, user_want, got_user)
    stats = jnp.concatenate([top, norm]).reshape(1, 1, -1)
    stats = jnp.broadcast_to(stats, (devices, 1, stats.shape[-1]))
    stats = jnp.pad(stats, ((0, 0), (0, 0), (0, -stats.shape[-1] % width)))
    stats = stats.reshape(devices, -1, width)
    user_parts = user_part.reshape(devices, -1, width)
    n_stat = stats.shape[1]
    got_s = lax.all_to_all(
        jnp.concatenate([stats, user_parts], axis=1), AXES, split_axis=0, concat_axis=0, tiled=True
    )
    flat_stats = got_s[:, :n_stat].reshape(devices, -1)
    top_all = flat_stats[:, :samples].reshape(total)
    norm_all = flat_stats[:, samples : 2 * samples].reshape(total)
    user_red = jnp.sum(got_s[:, n_stat:], 0)
    d_vn = scale / total * column_side(myself * samples, scale, vh, uh_all, top_all, norm_all)
    d_v = rv * (d_vn - vn * jnp.sum(vn * d_vn, -1, keepdims=True))
    goods_part = jnp.dot(item_emb.astype(jnp.float32).T, d_v, precision=highest)
    d_v_slot = jnp.dot(item_pick.T.astype(jnp.float32), d_v, precision=highest)
    goods_parts = jnp.transpose(goods_part.reshape(devices, -1, width), (1, 0, 2))
    chunk = goods_parts.shape[0]
    hi = goods_parts.astype(jnp.bfloat16)
    lo = (goods_parts - hi.astype(jnp.float32)).astype(jnp.bfloat16)
    send = jnp.concatenate(
        [d_v_slot.astype(jnp.bfloat16).reshape(cap_item, devices, width), hi, lo], axis=0
    )
    got = exchange(send)
    tail = got[cap_item:].astype(jnp.float32)
    goods_red = jnp.sum(tail[:chunk] + tail[chunk:], 1)
    red = jnp.concatenate([user_red, goods_red])
    spread = lax.all_to_all(
        jnp.broadcast_to(red[None], (devices,) + red.shape), AXES, split_axis=0, concat_axis=0, tiled=True
    )
    user_proj_grad = spread[:, :chunk].reshape(width, width)
    item_proj_grad = spread[:, chunk:].reshape(width, width)
    item_grad = add_rows(rows_dev, goods_want, got[:cap_item])
    return (user_grad, item_grad, user_proj_grad, item_proj_grad)


def solution(mesh):
    in_specs = (
        P(AXES, None),
        P(AXES, None),
        P(AXES, None),
        P(AXES),
        P(AXES, None),
        P(AXES),
        P(),
        P(AXES, None),
        P(AXES),
        P(),
        P(),
        P(),
    )
    out_specs = (P(AXES, None), P(AXES, None), P(), P())
    return jax.shard_map(local, mesh=mesh, in_specs=in_specs, out_specs=out_specs, check_vma=False)
```

```python
import jax
import jax.numpy as jnp
from jax import lax
from jax.sharding import PartitionSpec as P

EPS = 1e-06
AXES = ("dp", "table")


def tower(x, weight):
    u = jnp.dot(x, weight, preferred_element_type=jnp.float32)
    r = lax.rsqrt(jnp.sum(u * u, -1, keepdims=True) + EPS)
    return (u * r, r)


def slot_rank(owner, devices):
    onehot = (owner[:, None] == jnp.arange(devices, dtype=jnp.int32)[None, :]).astype(jnp.int32)
    before = jnp.cumsum(onehot, 0) - onehot
    return jnp.sum(before * onehot, 1)


def pick_rows(table, wanted):
    rows_dev = table.shape[0]
    flat = wanted.reshape(-1)
    onehot = (flat[:, None] == jnp.arange(rows_dev, dtype=jnp.int32)[None, :]).astype(table.dtype)
    picked = jnp.dot(onehot, table, preferred_element_type=jnp.float32).astype(table.dtype)
    return picked.reshape(wanted.shape + table.shape[1:])


def add_rows(rows_dev, wanted, values):
    flat = wanted.reshape(-1)
    onehot = (jnp.arange(rows_dev, dtype=jnp.int32)[:, None] == flat[None, :]).astype(values.dtype)
    return jnp.dot(onehot, values.reshape(flat.shape[0], -1), preferred_element_type=jnp.float32)


def exchange(x):
    return lax.all_to_all(x, AXES, split_axis=1, concat_axis=1, tiled=True)


def local(
    user_table,
    item_table,
    hist_owner,
    hist_row,
    hist_seg,
    hist_wix,
    bag_weights,
    item_owner,
    item_row,
    user_proj,
    item_proj,
    logit_scale,
):
    rows_dev, width = user_table.shape
    n_dp = lax.axis_size("dp")
    n_tab = lax.axis_size("table")
    devices = n_dp * n_tab
    tokens = hist_row.shape[0]
    samples = item_row.shape[0]
    cap = max(2, 2 * tokens // devices)
    cap_item = max(2, 2 * samples // devices)
    slots = cap + cap_item
    myself = lax.axis_index(AXES)
    entries = bag_weights.shape[0]
    segment = hist_seg[0]
    sample_ids = jnp.arange(samples, dtype=jnp.int32)
    owner = jnp.concatenate([hist_owner[:, 0], item_owner[:, 0]])
    rank = jnp.concatenate(
        [slot_rank(hist_owner[:, 0], devices), cap + slot_rank(item_owner[:, 0], devices)]
    )
    row = jnp.concatenate([hist_row, item_row])
    fields = jnp.stack(
        [
            row & 255,
            row >> 8,
            jnp.concatenate([segment, sample_ids]),
            jnp.concatenate([hist_wix, jnp.zeros((samples,), jnp.int32)]),
            jnp.ones_like(row),
        ]
    )
    by_owner = (owner[None, :] == jnp.arange(devices, dtype=jnp.int32)[:, None]).astype(jnp.bfloat16)
    planes = (fields.astype(jnp.bfloat16)[:, None, :] * by_owner[None, :, :]).reshape(-1, owner.shape[0])
    by_rank = (rank[:, None] == jnp.arange(slots, dtype=jnp.int32)[None, :]).astype(jnp.bfloat16)
    table = jnp.dot(planes, by_rank, preferred_element_type=jnp.float32)
    table = table.astype(jnp.int32).reshape(fields.shape[0], devices, slots)
    table = jnp.transpose(table, (0, 2, 1)).reshape(fields.shape[0], slots * devices)
    slot_row = table[0] + 256 * table[1]
    slot_seg = table[2]
    slot_wix = table[3]
    filled = table[4] > 0
    req = jnp.where(filled, slot_row, rows_dev).reshape(slots, devices)
    is_user = jnp.arange(slots * devices, dtype=jnp.int32) < cap * devices
    want = exchange(req)
    user_want = want[:cap]
    goods_want = want[cap:]
    goods_back = exchange(pick_rows(item_table, goods_want))
    user_back = exchange(pick_rows(user_table, user_want))
    wts = jnp.sum(
        jnp.where(
            slot_wix[:, None] == jnp.arange(entries, dtype=jnp.int32)[None, :],
            bag_weights[None, :].astype(jnp.float32),
            0.0,
        ),
        1,
    ).astype(jnp.bfloat16)
    of_sample = filled[None, :] & (slot_seg[None, :] == sample_ids[:, None])
    item_pick = of_sample[:, cap * devices :].astype(jnp.bfloat16)
    item_emb = jnp.dot(
        item_pick, goods_back.reshape(-1, width), preferred_element_type=jnp.float32
    ).astype(jnp.bfloat16)
    vn, rv = tower(item_emb, item_proj)
    vh = vn.astype(jnp.bfloat16)
    vh_all = lax.all_gather(vh, AXES, axis=0, tiled=True)
    coef = jnp.where(of_sample[:, : cap * devices], wts[None, : cap * devices], jnp.zeros((), jnp.bfloat16))
    numer = jnp.dot(coef, user_back.reshape(-1, width), preferred_element_type=jnp.float32)
    denom = jnp.sum(coef.astype(jnp.float32), 1)
    bag = (numer / denom[:, None]).astype(jnp.bfloat16)
    un, ru = tower(bag, user_proj)
    uh = un.astype(jnp.bfloat16)
    uh_all = lax.all_gather(uh, AXES, axis=0, tiled=True)
    scale = logit_scale[0]
    total = vh_all.shape[0]
    mine = myself * samples + sample_ids
    everyone = jnp.arange(total, dtype=jnp.int32)
    scores = scale * jnp.dot(uh, vh_all.T, preferred_element_type=jnp.float32)
    top = jnp.max(scores, -1)
    expo = jnp.exp(scores - top[:, None])
    norm = jnp.sum(expo, -1)
    prob = expo / norm[:, None]
    hot = (everyone[None, :] == mine[:, None]).astype(jnp.float32)
    pw = (prob - hot).astype(jnp.bfloat16)
    d_un = scale / total * jnp.dot(pw, vh_all, preferred_element_type=jnp.float32)
    d_u = ru * (d_un - un * jnp.sum(un * d_un, -1, keepdims=True))
    highest = lax.Precision.HIGHEST
    user_part = jnp.dot(bag.astype(jnp.float32).T, d_u, precision=highest)
    d_bag = jnp.dot(d_u, user_proj.astype(jnp.float32).T, precision=highest)
    n_user = cap * devices
    pick = jnp.concatenate([d_bag, denom[:, None]], axis=1)
    per_slot = jnp.dot(of_sample[:, :n_user].T.astype(jnp.float32), pick, precision=highest)
    g_slot = (wts[:n_user].astype(jnp.float32) / per_slot[:, width])[:, None] * per_slot[:, :width]
    g_slot = jnp.where(filled[:n_user, None], g_slot, 0.0)
    got_user = exchange(g_slot.astype(jnp.bfloat16).reshape(cap, devices, width))
    user_grad = add_rows(rows_dev, user_want, got_user)
    stats = jnp.concatenate([top, norm]).reshape(1, 1, -1)
    stats = jnp.broadcast_to(stats, (devices, 1, stats.shape[-1]))
    stats = jnp.pad(stats, ((0, 0), (0, 0), (0, -stats.shape[-1] % width)))
    stats = stats.reshape(devices, -1, width)
    user_parts = user_part.reshape(devices, -1, width)
    n_stat = stats.shape[1]
    got_s = lax.all_to_all(
        jnp.concatenate([stats, user_parts], axis=1), AXES, split_axis=0, concat_axis=0, tiled=True
    )
    flat_stats = got_s[:, :n_stat].reshape(devices, -1)
    top_all = flat_stats[:, :samples].reshape(total)
    norm_all = flat_stats[:, samples : 2 * samples].reshape(total)
    user_red = jnp.sum(got_s[:, n_stat:], 0)
    uh_all, user_grad = lax.optimization_barrier((uh_all, user_grad))
    scores_c = scale * jnp.dot(vh, uh_all.T, preferred_element_type=jnp.float32)
    prob_c = jnp.exp(scores_c - top_all[None, :]) / norm_all[None, :]
    hot_c = (everyone[None, :] == mine[:, None]).astype(jnp.float32)
    pw_c = (prob_c - hot_c).astype(jnp.bfloat16)
    d_vn = scale / total * jnp.dot(pw_c, uh_all, preferred_element_type=jnp.float32)
    d_v = rv * (d_vn - vn * jnp.sum(vn * d_vn, -1, keepdims=True))
    goods_part = jnp.dot(item_emb.astype(jnp.float32).T, d_v, precision=highest)
    d_v_slot = jnp.dot(item_pick.T.astype(jnp.float32), d_v, precision=highest)
    goods_parts = jnp.transpose(goods_part.reshape(devices, -1, width), (1, 0, 2))
    chunk = goods_parts.shape[0]
    hi = goods_parts.astype(jnp.bfloat16)
    lo = (goods_parts - hi.astype(jnp.float32)).astype(jnp.bfloat16)
    send = jnp.concatenate(
        [d_v_slot.astype(jnp.bfloat16).reshape(cap_item, devices, width), hi, lo], axis=0
    )
    got = exchange(send)
    tail = got[cap_item:].astype(jnp.float32)
    goods_red = jnp.sum(tail[:chunk] + tail[chunk:], 1)
    red = jnp.concatenate([user_red, goods_red])
    spread = lax.all_to_all(
        jnp.broadcast_to(red[None], (devices,) + red.shape), AXES, split_axis=0, concat_axis=0, tiled=True
    )
    user_proj_grad = spread[:, :chunk].reshape(width, width)
    item_proj_grad = spread[:, chunk:].reshape(width, width)
    item_grad = add_rows(rows_dev, goods_want, got[:cap_item])
    return (user_grad, item_grad, user_proj_grad, item_proj_grad)


def solution(mesh):
    in_specs = (
        P(AXES, None),
        P(AXES, None),
        P(AXES, None),
        P(AXES),
        P(AXES, None),
        P(AXES),
        P(),
        P(AXES, None),
        P(AXES),
        P(),
        P(),
        P(),
    )
    out_specs = (P(AXES, None), P(AXES, None), P(), P())
    return jax.shard_map(local, mesh=mesh, in_specs=in_specs, out_specs=out_specs, check_vma=False)
```

```python
import jax
import jax.numpy as jnp
from jax import lax
from jax.sharding import PartitionSpec as P

EPS = 1e-06
AXES = ("dp", "table")


def tower(x, weight):
    u = jnp.dot(x, weight, preferred_element_type=jnp.float32)
    r = lax.rsqrt(jnp.sum(u * u, -1, keepdims=True) + EPS)
    return (u * r, r)


def slot_rank(owner, devices):
    onehot = (owner[:, None] == jnp.arange(devices, dtype=jnp.int32)[None, :]).astype(jnp.int32)
    before = jnp.cumsum(onehot, 0) - onehot
    return jnp.sum(before * onehot, 1)


def pick_rows(table, wanted):
    rows_dev = table.shape[0]
    flat = wanted.reshape(-1)
    onehot = (flat[:, None] == jnp.arange(rows_dev, dtype=jnp.int32)[None, :]).astype(table.dtype)
    picked = jnp.dot(onehot, table, preferred_element_type=jnp.float32).astype(table.dtype)
    return picked.reshape(wanted.shape + table.shape[1:])


def add_rows(rows_dev, wanted, values):
    flat = wanted.reshape(-1)
    onehot = (jnp.arange(rows_dev, dtype=jnp.int32)[:, None] == flat[None, :]).astype(values.dtype)
    return jnp.dot(onehot, values.reshape(flat.shape[0], -1), preferred_element_type=jnp.float32)


def exchange(x):
    return lax.all_to_all(x, AXES, split_axis=1, concat_axis=1, tiled=True)


def local(
    user_table,
    item_table,
    hist_owner,
    hist_row,
    hist_seg,
    hist_wix,
    bag_weights,
    item_owner,
    item_row,
    user_proj,
    item_proj,
    logit_scale,
):
    rows_dev, width = user_table.shape
    n_dp = lax.axis_size("dp")
    n_tab = lax.axis_size("table")
    devices = n_dp * n_tab
    tokens = hist_row.shape[0]
    samples = item_row.shape[0]
    cap = max(2, 2 * tokens // devices)
    cap_item = max(2, 2 * samples // devices)
    slots = cap + cap_item
    myself = lax.axis_index(AXES)
    entries = bag_weights.shape[0]
    segment = hist_seg[0]
    sample_ids = jnp.arange(samples, dtype=jnp.int32)
    owner = jnp.concatenate([hist_owner[:, 0], item_owner[:, 0]])
    rank = jnp.concatenate(
        [slot_rank(hist_owner[:, 0], devices), cap + slot_rank(item_owner[:, 0], devices)]
    )
    row = jnp.concatenate([hist_row, item_row])
    fields = jnp.stack(
        [
            row & 255,
            row >> 8,
            jnp.concatenate([segment, sample_ids]),
            jnp.concatenate([hist_wix, jnp.zeros((samples,), jnp.int32)]),
            jnp.ones_like(row),
        ]
    )
    by_owner = (owner[None, :] == jnp.arange(devices, dtype=jnp.int32)[:, None]).astype(jnp.bfloat16)
    planes = (fields.astype(jnp.bfloat16)[:, None, :] * by_owner[None, :, :]).reshape(-1, owner.shape[0])
    by_rank = (rank[:, None] == jnp.arange(slots, dtype=jnp.int32)[None, :]).astype(jnp.bfloat16)
    table = jnp.dot(planes, by_rank, preferred_element_type=jnp.float32)
    table = table.astype(jnp.int32).reshape(fields.shape[0], devices, slots)
    table = jnp.transpose(table, (0, 2, 1)).reshape(fields.shape[0], slots * devices)
    slot_row = table[0] + 256 * table[1]
    slot_seg = table[2]
    slot_wix = table[3]
    filled = table[4] > 0
    req = jnp.where(filled, slot_row, rows_dev).reshape(slots, devices)
    is_user = jnp.arange(slots * devices, dtype=jnp.int32) < cap * devices
    want = exchange(req)
    user_want = want[:cap]
    goods_want = want[cap:]
    goods_back = exchange(pick_rows(item_table, goods_want))
    user_back = exchange(pick_rows(user_table, user_want))
    wts = jnp.sum(
        jnp.where(
            slot_wix[:, None] == jnp.arange(entries, dtype=jnp.int32)[None, :],
            bag_weights[None, :].astype(jnp.float32),
            0.0,
        ),
        1,
    ).astype(jnp.bfloat16)
    of_sample = filled[None, :] & (slot_seg[None, :] == sample_ids[:, None])
    item_pick = of_sample[:, cap * devices :].astype(jnp.bfloat16)
    item_emb = jnp.dot(
        item_pick, goods_back.reshape(-1, width), preferred_element_type=jnp.float32
    ).astype(jnp.bfloat16)
    vn, rv = tower(item_emb, item_proj)
    vh = vn.astype(jnp.bfloat16)
    vh_all = lax.all_gather(vh, AXES, axis=0, tiled=True)
    coef = jnp.where(of_sample[:, : cap * devices], wts[None, : cap * devices], jnp.zeros((), jnp.bfloat16))
    numer = jnp.dot(coef, user_back.reshape(-1, width), preferred_element_type=jnp.float32)
    denom = jnp.sum(coef.astype(jnp.float32), 1)
    bag = (numer / denom[:, None]).astype(jnp.bfloat16)
    un, ru = tower(bag, user_proj)
    uh = un.astype(jnp.bfloat16)
    uh_all = lax.all_gather(uh, AXES, axis=0, tiled=True)
    scale = logit_scale[0]
    total = vh_all.shape[0]
    mine = myself * samples + sample_ids
    everyone = jnp.arange(total, dtype=jnp.int32)
    scores = scale * jnp.dot(uh, vh_all.T, preferred_element_type=jnp.float32)
    top = jnp.max(scores, -1)
    expo = jnp.exp(scores - top[:, None])
    norm = jnp.sum(expo, -1)
    prob = expo / norm[:, None]
    hot = (everyone[None, :] == mine[:, None]).astype(jnp.float32)
    pw = (prob - hot).astype(jnp.bfloat16)
    d_un = scale / total * jnp.dot(pw, vh_all, preferred_element_type=jnp.float32)
    d_u = ru * (d_un - un * jnp.sum(un * d_un, -1, keepdims=True))
    highest = lax.Precision.HIGHEST
    user_part = jnp.dot(bag.astype(jnp.float32).T, d_u, precision=highest)
    d_bag = jnp.dot(d_u, user_proj.astype(jnp.float32).T, precision=highest)
    n_user = cap * devices
    pick = jnp.concatenate([d_bag, denom[:, None]], axis=1)
    per_slot = jnp.dot(of_sample[:, :n_user].T.astype(jnp.float32), pick, precision=highest)
    g_slot = (wts[:n_user].astype(jnp.float32) / per_slot[:, width])[:, None] * per_slot[:, :width]
    g_slot = jnp.where(filled[:n_user, None], g_slot, 0.0)
    stats = jnp.concatenate([top, norm]).reshape(1, 1, -1)
    stats = jnp.broadcast_to(stats, (devices, 1, stats.shape[-1]))
    stats = jnp.pad(stats, ((0, 0), (0, 0), (0, -stats.shape[-1] % width)))
    stats = stats.reshape(devices, -1, width)
    user_parts = user_part.reshape(devices, -1, width)
    n_stat = stats.shape[1]
    got_s = lax.all_to_all(
        jnp.concatenate([stats, user_parts], axis=1), AXES, split_axis=0, concat_axis=0, tiled=True
    )
    flat_stats = got_s[:, :n_stat].reshape(devices, -1)
    top_all = flat_stats[:, :samples].reshape(total)
    norm_all = flat_stats[:, samples : 2 * samples].reshape(total)
    user_red = jnp.sum(got_s[:, n_stat:], 0)
    pieces = []
    rest = user_red
    for _ in range(3):
        piece = rest.astype(jnp.bfloat16)
        pieces.append(piece)
        rest = rest - piece.astype(jnp.float32)
    pieces = jnp.concatenate(pieces)
    n_piece = pieces.shape[0]
    got_user = exchange(
        jnp.concatenate(
            [
                g_slot.astype(jnp.bfloat16).reshape(cap, devices, width),
                jnp.broadcast_to(pieces[:, None], (n_piece, devices, width)),
            ]
        )
    )
    chunk_u = user_red.shape[0]
    spread_u = got_user[cap:].astype(jnp.float32).reshape(3, chunk_u, devices, width).sum(0)
    user_proj_grad = jnp.transpose(spread_u, (1, 0, 2)).reshape(width, width)
    user_grad = add_rows(rows_dev, user_want, got_user[:cap])
    scores_c = scale * jnp.dot(vh, uh_all.T, preferred_element_type=jnp.float32)
    prob_c = jnp.exp(scores_c - top_all[None, :]) / norm_all[None, :]
    hot_c = (everyone[None, :] == mine[:, None]).astype(jnp.float32)
    pw_c = (prob_c - hot_c).astype(jnp.bfloat16)
    d_vn = scale / total * jnp.dot(pw_c, uh_all, preferred_element_type=jnp.float32)
    d_v = rv * (d_vn - vn * jnp.sum(vn * d_vn, -1, keepdims=True))
    goods_part = jnp.dot(item_emb.astype(jnp.float32).T, d_v, precision=highest)
    d_v_slot = jnp.dot(item_pick.T.astype(jnp.float32), d_v, precision=highest)
    goods_parts = jnp.transpose(goods_part.reshape(devices, -1, width), (1, 0, 2))
    chunk = goods_parts.shape[0]
    hi = goods_parts.astype(jnp.bfloat16)
    lo = (goods_parts - hi.astype(jnp.float32)).astype(jnp.bfloat16)
    send = jnp.concatenate(
        [d_v_slot.astype(jnp.bfloat16).reshape(cap_item, devices, width), hi, lo], axis=0
    )
    got = exchange(send)
    tail = got[cap_item:].astype(jnp.float32)
    goods_red = jnp.sum(tail[:chunk] + tail[chunk:], 1)
    spread = lax.all_to_all(
        jnp.broadcast_to(goods_red[None], (devices,) + goods_red.shape), AXES, split_axis=0, concat_axis=0, tiled=True
    )
    item_proj_grad = spread.reshape(width, width)
    item_grad = add_rows(rows_dev, goods_want, got[:cap_item])
    return (user_grad, item_grad, user_proj_grad, item_proj_grad)


def solution(mesh):
    in_specs = (
        P(AXES, None),
        P(AXES, None),
        P(AXES, None),
        P(AXES),
        P(AXES, None),
        P(AXES),
        P(),
        P(AXES, None),
        P(AXES),
        P(),
        P(),
        P(),
    )
    out_specs = (P(AXES, None), P(AXES, None), P(), P())
    return jax.shard_map(local, mesh=mesh, in_specs=in_specs, out_specs=out_specs, check_vma=False)
```
